128 devices in a mesh: guid: 2 (over x_hi), req: 4 (over x_lo, core), seq: 16 (over y, z).
Axes of the slice: x: 4 (x_hi: 2, x_lo: 2; x = x_hi * 2 + x_lo), y: 4, z: 4, core: 2. Of those that a mesh axis runs over, the one named last changes fastest.
Arguments:
- img_hidden: bfloat16 [2, 24, 1024, 1536], P('guid', 'req', 'seq'), may hold values from -6 to 6
- txt_hidden: bfloat16 [2, 24, 192, 1536], P('guid', 'req', 'seq'), may hold values from -6 to 6
- img_mod: float32 [2, 24, 5, 1536], P('guid', 'req')
- txt_mod: float32 [2, 24, 2, 1536], P('guid', 'req'), may hold values from -3 to 3
- w_img_qkv: bfloat16 [1536, 3072], P(('guid', 'req', 'seq')), may hold values from -0.15625 to 0.15625
- w_txt_qkv: bfloat16 [1536, 3072], P(('guid', 'req', 'seq')), may hold values from -0.15625 to 0.15625
- w_out: bfloat16 [1024, 1536], P(('guid', 'req', 'seq')), may hold values from -0.1875 to 0.1875
- w_head: bfloat16 [1536, 64], P(('guid', 'req', 'seq')), may hold values from -0.15625 to 0.15625
- text_lengths: int32 [2, 24], P('guid', 'req'), may hold values from 1 to 154, as said below
- latent: float32 [24, 1024, 64], P('req', 'seq', 'guid'), may hold values from -6 to 6
- step: int32 [1], replicated, may hold values from 0 to 27
Outputs:
- advanced: float32 [24, 1024, 64], P('req', 'seq', 'guid')
- guided: float32 [24, 1024, 64], P('req', 'seq', 'guid')
The draws below stay inside these ranges and needn't reach their ends.
Inputs may be any that keep to these rules, and one draw needn't show every extreme that they name: `text_lengths`: in each half one prompt has 154 text tokens and another has 1.
All inputs are finite; a program needn't handle non-finite values.
Results may differ from the reference program's by a relative error of at most 0.012.
The reference program's roundings to bfloat16 on the way count: a program that leaves them out, or rounds other values in their place, can miss the bound.
Values may be sent and summed in bfloat16 or wider, within the bound.
No kernel may reach another device: no remote copies, remote signals or barrier semaphores. Data moves between devices by JAX's collectives and lax.ppermute only.
A program may use at most 192 MiB of HBM per device.

```python
import jax
import jax.numpy as jnp
from jax import lax

D = 1536
HEADS = 16
HD = 64
IMG = 1024
TXT = 192
TXT_MAX = 154
PATCH = 64
STEPS = 28
PROMPTS = 24
AW = 1024


def draw_img_mod(key, part):
    sample = 0.5 * jax.random.normal(key, (2, PROMPTS, 5, D), jnp.float32)
    return sample


def draw_text_lengths(key, part):
    sample = jax.random.randint(key, (2, PROMPTS), 1, TXT_MAX + 1)
    chosen = jax.random.randint(jax.random.fold_in(key, 3), (2, 1), 0, PROMPTS)
    places = jnp.arange(PROMPTS)[None, :]
    sample = jnp.where(places == chosen, TXT_MAX, sample)
    sample = jnp.where(places == (chosen + 1) % PROMPTS, 1, sample)
    return sample.astype(jnp.int32)


def level_of(own_key, dims, cuts, least, high):
    factor_of = 1.0
    for axis_at, parts in cuts:
        heights = jax.random.uniform(jax.random.fold_in(jax.random.fold_in(own_key, 6), axis_at), (parts,), jnp.float32, least / len(cuts), high / len(cuts))
        factor_of = factor_of * jnp.repeat(jnp.exp(heights), dims[axis_at] // parts).reshape((-1,) + (1,) * (len(dims) - 1 - axis_at))
    return factor_of


def noise(own_key, shape, scale, limit, split=(), held_as=jnp.bfloat16):
    entries = scale * jax.random.normal(own_key, shape, jnp.float32)
    if split:
        entries = entries * level_of(own_key, shape, split, -0.22, 0.18)
    return jnp.clip(entries, -limit, limit).astype(held_as)


def setup_inputs(seed: int = 0) -> dict:
    keys = jax.random.split(jax.random.key(seed), 12)
    return {
        "img_hidden": noise(keys[0], (2, PROMPTS, IMG, D), 1.0, 6.0, ((0, 2), (1, 4), (2, 16))),
        "txt_hidden": noise(keys[1], (2, PROMPTS, TXT, D), 1.0, 6.0, ((0, 2), (1, 4), (2, 16))),
        "img_mod": draw_img_mod(jax.random.fold_in(keys[11], 71), 0),
        "txt_mod": noise(keys[3], (2, PROMPTS, 2, D), 0.5, 3.0, ((0, 2), (1, 4)), jnp.float32),
        "w_img_qkv": noise(keys[4], (D, 3 * AW), D ** -0.5, 0.15625, ((0, 128),)),
        "w_txt_qkv": noise(keys[5], (D, 3 * AW), D ** -0.5, 0.15625, ((0, 128),)),
        "w_out": noise(keys[6], (AW, D), AW ** -0.5, 0.1875, ((0, 128),)),
        "w_head": noise(keys[7], (D, PATCH), D ** -0.5, 0.15625, ((0, 128),)),
        "text_lengths": draw_text_lengths(jax.random.fold_in(keys[11], 71), 0),
        "latent": noise(keys[9], (PROMPTS, IMG, PATCH), 1.0, 6.0, ((0, 4), (1, 16), (2, 2)), jnp.float32),
        "step": jax.random.randint(keys[10], (1,), 0, STEPS).astype(jnp.int32),
    }


norm_epsilon = 1e-06
flow_shift = 3.0
guide_scale = 4.5

def modulate(values_in, shift_vec, scale_vec):
    values_in = values_in.astype(jnp.float32)
    average = lax.optimization_barrier(jnp.mean(values_in, axis=-1, keepdims=True))
    variance = lax.optimization_barrier(jnp.mean((values_in - average) ** 2, axis=-1, keepdims=True))
    normed = (values_in - average) * lax.rsqrt(variance + norm_epsilon)
    return (normed * (1.0 + scale_vec[..., None, :]) + shift_vec[..., None, :]).astype(jnp.bfloat16)

def sigma_level(step_value):
    remaining = 1.0 - step_value / STEPS
    return flow_shift * remaining / (1.0 + (flow_shift - 1.0) * remaining)

def reference(img_hidden, txt_hidden, img_mod, txt_mod, w_img_qkv, w_txt_qkv, w_out, w_head, text_lengths, latent, step):
    attn_width = w_out.shape[0]
    image_in = modulate(img_hidden, img_mod[:, :, 0], img_mod[:, :, 1])
    text_in = modulate(txt_hidden, txt_mod[:, :, 0], txt_mod[:, :, 1])

    def per_prompt(members):
        image_rows, text_rows, modulation, hidden, length = members
        qkv_image = lax.optimization_barrier(jnp.dot(image_rows, w_img_qkv, preferred_element_type=jnp.float32).astype(jnp.bfloat16))
        qkv_text = lax.optimization_barrier(jnp.dot(text_rows, w_txt_qkv, preferred_element_type=jnp.float32).astype(jnp.bfloat16))
        query_rows = qkv_image[:, :attn_width].astype(jnp.float32).reshape(IMG, HEADS, HD)
        key_rows = jnp.concatenate([qkv_image[:, attn_width:2 * attn_width], qkv_text[:, attn_width:2 * attn_width]], axis=0)
        value_rows = jnp.concatenate([qkv_image[:, 2 * attn_width:], qkv_text[:, 2 * attn_width:]], axis=0)
        key_rows = key_rows.astype(jnp.float32).reshape(IMG + TXT, HEADS, HD)
        value_rows = value_rows.astype(jnp.float32).reshape(IMG + TXT, HEADS, HD)
        allowed = jnp.concatenate([jnp.ones((IMG,), bool), jnp.arange(TXT, dtype=jnp.int32) < length])
        scores = jnp.einsum('qhd,khd->hqk', query_rows, key_rows) * 0.125
        scores = jnp.where(allowed[None, None, :], scores, -1e+30)
        highest = lax.optimization_barrier(jnp.max(scores, axis=-1, keepdims=True))
        weights = jnp.exp(scores - highest)
        totals = lax.optimization_barrier(jnp.sum(weights, axis=-1))
        rounded = lax.optimization_barrier(weights.astype(jnp.bfloat16)).astype(jnp.float32)
        mixture = jnp.einsum('hqk,khd->qhd', rounded, value_rows) / jnp.transpose(totals)[:, :, None]
        attended = mixture.reshape(IMG, attn_width).astype(jnp.bfloat16)
        projected = jnp.dot(attended, w_out, preferred_element_type=jnp.float32)
        residual = hidden.astype(jnp.float32) + modulation[2][None, :] * projected
        final_in = modulate(residual, modulation[3], modulation[4])
        return jnp.dot(final_in, w_head, preferred_element_type=jnp.float32)
    count_all = 2 * PROMPTS
    velocity = lax.map(per_prompt, (image_in.reshape(count_all, IMG, D), text_in.reshape(count_all, TXT, D), img_mod.reshape(count_all, 5, D), img_hidden.reshape(count_all, IMG, D), text_lengths.reshape(count_all)))
    velocity = velocity.reshape(2, PROMPTS, IMG, PATCH)
    guided = velocity[1] + guide_scale * (velocity[0] - velocity[1])
    step_value = step[0].astype(jnp.float32)
    advanced = latent + (sigma_level(step_value + 1.0) - sigma_level(step_value)) * guided
    return (advanced, guided)
```

```python
import jax
import jax.numpy as jnp
from jax import lax
from jax.sharding import PartitionSpec as P

HD = 64
STEPS = 28


norm_epsilon = 1e-06
flow_shift = 3.0
guide_scale = 4.5


def partner(value, axis, bit):
    mask = 2**bit
    pairs = [(source, source ^ mask) for source in range(lax.axis_size(axis))]
    return lax.ppermute(value, axis, pairs)


def modulate(values_in, shift_vec, scale_vec):
    values_in = values_in.astype(jnp.float32)
    average = jnp.mean(values_in, axis=-1, keepdims=True)
    variance = jnp.mean((values_in - average) ** 2, axis=-1, keepdims=True)
    normed = (values_in - average) * lax.rsqrt(variance + norm_epsilon)
    return (normed * (1.0 + scale_vec[..., None, :]) + shift_vec[..., None, :]).astype(jnp.bfloat16)


def sigma_level(step_value):
    remaining = 1.0 - step_value / STEPS
    return flow_shift * remaining / (1.0 + (flow_shift - 1.0) * remaining)


def local(
    img_hidden,
    txt_hidden,
    img_mod,
    txt_mod,
    w_img_qkv,
    w_txt_qkv,
    w_out,
    w_head,
    text_lengths,
    latent,
    step,
):
    all_axes = ("guid", "req", "seq")
    prompts = img_hidden.shape[1]
    img_rows = img_hidden.shape[2]
    txt_rows = txt_hidden.shape[2]
    model_width = img_hidden.shape[3]
    nseq = lax.axis_size("seq")

    full_img = lax.all_gather(w_img_qkv, all_axes, axis=0, tiled=True)
    full_txt = lax.all_gather(w_txt_qkv, all_axes, axis=0, tiled=True)
    head_rows, head_cols = w_head.shape
    full_head = lax.all_gather(
        w_head.reshape(1, head_rows * head_cols), all_axes, axis=0, tiled=True
    ).reshape(-1, head_cols)
    full_out = lax.all_gather(w_out, all_axes, axis=0, tiled=True)

    image_in = modulate(img_hidden[0], img_mod[0, :, 0], img_mod[0, :, 1])
    text_in = modulate(txt_hidden[0], txt_mod[0, :, 0], txt_mod[0, :, 1])
    attn_width = full_img.shape[1] // 3
    head_count = attn_width // HD
    per_dev = head_count // nseq
    qkv_image = jnp.einsum(
        "prd,de->pre", image_in, full_img, preferred_element_type=jnp.float32
    ).astype(jnp.bfloat16)
    qkv_text = jnp.einsum(
        "prd,de->pre", text_in, full_txt, preferred_element_type=jnp.float32
    ).astype(jnp.bfloat16)

    img_split = qkv_image.reshape(prompts, img_rows, 3, nseq, per_dev * HD)
    img_heads = lax.all_to_all(img_split, "seq", 3, 1, tiled=True)
    txt_split = qkv_text[..., attn_width:].reshape(prompts, txt_rows, 2, nseq, per_dev * HD)
    txt_heads = lax.all_to_all(txt_split, "seq", 3, 1, tiled=True)
    all_img = img_heads.shape[1]
    all_txt = txt_heads.shape[1]

    query_heads = img_heads[:, :, 0, 0].reshape(prompts, all_img, per_dev, HD)
    key_heads = jnp.concatenate(
        [img_heads[:, :, 1, 0], txt_heads[:, :, 0, 0]], axis=1
    ).reshape(prompts, all_img + all_txt, per_dev, HD)
    value_heads = jnp.concatenate(
        [img_heads[:, :, 2, 0], txt_heads[:, :, 1, 0]], axis=1
    ).reshape(prompts, all_img + all_txt, per_dev, HD)

    lengths = text_lengths[0]
    scores = (
        jnp.einsum("pqhd,pkhd->phqk", query_heads, key_heads, preferred_element_type=jnp.float32)
        * 0.125
    )
    position = jnp.arange(all_img + all_txt, dtype=jnp.int32)
    allowed = (position < all_img)[None, :] | ((position - all_img)[None, :] < lengths[:, None])
    scores = jnp.where(allowed[:, None, None, :], scores, -1e30)
    highest = jnp.max(scores, axis=-1)
    weights = jnp.exp(scores - highest[..., None])
    totals = jnp.sum(weights, axis=-1)
    accumulated = jnp.einsum(
        "phqk,pkhd->pqhd",
        weights.astype(jnp.bfloat16),
        value_heads,
        preferred_element_type=jnp.float32,
    )
    mixture = accumulated / jnp.transpose(totals, (0, 2, 1))[..., None]
    head_out = mixture.astype(jnp.bfloat16).reshape(prompts, all_img, 1, per_dev * HD)
    token_out = lax.all_to_all(head_out, "seq", 1, 2, tiled=True)
    attended = token_out.reshape(prompts * img_rows, attn_width)

    projected = jnp.dot(attended, full_out, preferred_element_type=jnp.float32)
    residual = img_hidden[0].astype(jnp.float32) + img_mod[0, :, 2][:, None, :] * projected.reshape(
        prompts, img_rows, model_width
    )
    final_in = modulate(residual, img_mod[0, :, 3], img_mod[0, :, 4])
    guid_index = lax.axis_index("guid")
    half_width = latent.shape[2]
    own_start = guid_index * half_width
    other_start = (1 - guid_index) * half_width
    whole_velocity = jnp.einsum(
        "prd,dc->prc", final_in, full_head, preferred_element_type=jnp.float32
    )
    own_velocity = lax.dynamic_slice_in_dim(whole_velocity, own_start, half_width, 2)
    partner_part = lax.dynamic_slice_in_dim(whole_velocity, other_start, half_width, 2)
    other_velocity = partner(partner_part.astype(jnp.bfloat16), "guid", 0).astype(
        partner_part.dtype
    )
    cond_velocity = jnp.where(guid_index == 0, own_velocity, other_velocity)
    free_velocity = jnp.where(guid_index == 0, other_velocity, own_velocity)
    guided = free_velocity + guide_scale * (cond_velocity - free_velocity)
    step_value = step[0].astype(jnp.float32)
    advanced = latent + (sigma_level(step_value + 1.0) - sigma_level(step_value)) * guided
    return (advanced, guided)


def solution(mesh):
    placed = (
        P("guid", "req", "seq", None),
        P("guid", "req", "seq", None),
        P("guid", "req", None, None),
        P("guid", "req", None, None),
        P(("guid", "req", "seq"), None),
        P(("guid", "req", "seq"), None),
        P(("guid", "req", "seq"), None),
        P(("guid", "req", "seq"), None),
        P("guid", "req"),
        P("req", "seq", "guid"),
        P(),
    )
    return jax.shard_map(
        local,
        mesh=mesh,
        in_specs=placed,
        out_specs=(P("req", "seq", "guid"), P("req", "seq", "guid")),
        check_vma=False,
    )
```

```python
import jax
import jax.numpy as jnp
from jax import lax
from jax.sharding import PartitionSpec as P

HD = 64
STEPS = 28


norm_epsilon = 1e-06
flow_shift = 3.0
guide_scale = 4.5


def partner(value, axis, bit):
    mask = 2**bit
    pairs = [(source, source ^ mask) for source in range(lax.axis_size(axis))]
    return lax.ppermute(value, axis, pairs)


def modulate(values_in, shift_vec, scale_vec):
    values_in = values_in.astype(jnp.float32)
    average = jnp.mean(values_in, axis=-1, keepdims=True)
    variance = jnp.mean((values_in - average) ** 2, axis=-1, keepdims=True)
    normed = (values_in - average) * lax.rsqrt(variance + norm_epsilon)
    return (normed * (1.0 + scale_vec[..., None, :]) + shift_vec[..., None, :]).astype(jnp.bfloat16)


def sigma_level(step_value):
    remaining = 1.0 - step_value / STEPS
    return flow_shift * remaining / (1.0 + (flow_shift - 1.0) * remaining)


def permute_columns(values):
    lead = values.shape[:-1]
    cores = lax.axis_size("core")
    outer = lax.axis_size("guid") * lax.axis_size("xlo")
    split = values.reshape(lead + (outer, cores, values.shape[-1] // (outer * cores)))
    n = len(lead)
    order = tuple(range(n)) + (n + 1, n, n + 2)
    return jnp.transpose(split, order).reshape(values.shape)


def local(
    img_hidden,
    txt_hidden,
    img_mod,
    txt_mod,
    w_img_qkv,
    w_txt_qkv,
    w_out,
    w_head,
    text_lengths,
    latent,
    step,
):
    all_axes = ("guid", "xlo", "core", "seq")
    prompts = img_hidden.shape[1]
    img_rows = img_hidden.shape[2]
    txt_rows = txt_hidden.shape[2]
    model_width = img_hidden.shape[3]
    nseq = lax.axis_size("seq")

    outer = ("guid", "xlo", "seq")
    full_img = lax.all_gather(
        lax.all_gather(w_img_qkv, outer, axis=0, tiled=True), "core", axis=0, tiled=True
    )
    full_txt = lax.all_gather(
        lax.all_gather(w_txt_qkv, outer, axis=0, tiled=True), "core", axis=0, tiled=True
    )
    out_rows, out_cols = w_out.shape
    head_rows, head_cols = w_head.shape
    head_flat = w_head.reshape(1, head_rows * head_cols)
    head_flat = jnp.pad(head_flat, ((0, 0), (0, out_cols - head_rows * head_cols)))
    packed = lax.all_gather(
        jnp.concatenate([w_out, head_flat], axis=0), all_axes, axis=0, tiled=False
    )
    full_out = packed[:, :out_rows].reshape(-1, out_cols)
    full_head = packed[:, out_rows, : head_rows * head_cols].reshape(-1, head_cols)

    image_in = permute_columns(modulate(img_hidden[0], img_mod[0, :, 0], img_mod[0, :, 1]))
    text_in = permute_columns(modulate(txt_hidden[0], txt_mod[0, :, 0], txt_mod[0, :, 1]))
    attn_width = full_img.shape[1] // 3
    head_count = attn_width // HD
    per_dev = head_count // nseq
    qkv_image = jnp.einsum(
        "prd,de->pre", image_in, full_img, preferred_element_type=jnp.float32
    ).astype(jnp.bfloat16)
    qkv_text = jnp.einsum(
        "prd,de->pre", text_in, full_txt, preferred_element_type=jnp.float32
    ).astype(jnp.bfloat16)

    img_split = qkv_image.reshape(prompts, img_rows, 3, nseq, per_dev * HD)
    img_heads = lax.all_to_all(img_split, "seq", 3, 1, tiled=True)
    txt_split = qkv_text[..., attn_width:].reshape(prompts, txt_rows, 2, nseq, per_dev * HD)
    txt_heads = lax.all_to_all(txt_split, "seq", 3, 1, tiled=True)
    all_img = img_heads.shape[1]
    all_txt = txt_heads.shape[1]

    query_heads = img_heads[:, :, 0, 0].reshape(prompts, all_img, per_dev, HD)
    key_heads = jnp.concatenate(
        [img_heads[:, :, 1, 0], txt_heads[:, :, 0, 0]], axis=1
    ).reshape(prompts, all_img + all_txt, per_dev, HD)
    value_heads = jnp.concatenate(
        [img_heads[:, :, 2, 0], txt_heads[:, :, 1, 0]], axis=1
    ).reshape(prompts, all_img + all_txt, per_dev, HD)

    lengths = text_lengths[0]
    scores = (
        jnp.einsum("pqhd,pkhd->phqk", query_heads, key_heads, preferred_element_type=jnp.float32)
        * 0.125
    )
    position = jnp.arange(all_img + all_txt, dtype=jnp.int32)
    allowed = (position < all_img)[None, :] | ((position - all_img)[None, :] < lengths[:, None])
    scores = jnp.where(allowed[:, None, None, :], scores, -1e30)
    highest = jnp.max(scores, axis=-1)
    weights = jnp.exp(scores - highest[..., None])
    totals = jnp.sum(weights, axis=-1)
    accumulated = jnp.einsum(
        "phqk,pkhd->pqhd",
        weights.astype(jnp.bfloat16),
        value_heads,
        preferred_element_type=jnp.float32,
    )
    mixture = accumulated / jnp.transpose(totals, (0, 2, 1))[..., None]
    head_out = mixture.astype(jnp.bfloat16).reshape(prompts, all_img, 1, per_dev * HD)
    token_out = lax.all_to_all(head_out, "seq", 1, 2, tiled=True)
    attended = token_out.reshape(prompts * img_rows, attn_width)

    projected = jnp.dot(attended, full_out, preferred_element_type=jnp.float32)
    residual = img_hidden[0].astype(jnp.float32) + img_mod[0, :, 2][:, None, :] * projected.reshape(
        prompts, img_rows, model_width
    )
    final_in = modulate(residual, img_mod[0, :, 3], img_mod[0, :, 4])
    guid_index = lax.axis_index("guid")
    half_width = latent.shape[2]
    own_start = guid_index * half_width
    other_start = (1 - guid_index) * half_width
    whole_velocity = jnp.einsum(
        "prd,dc->prc", final_in, full_head, preferred_element_type=jnp.float32
    )
    own_velocity = lax.dynamic_slice_in_dim(whole_velocity, own_start, half_width, 2)
    partner_part = lax.dynamic_slice_in_dim(whole_velocity, other_start, half_width, 2)
    other_velocity = partner(partner_part.astype(jnp.bfloat16), "guid", 0).astype(
        partner_part.dtype
    )
    cond_velocity = jnp.where(guid_index == 0, own_velocity, other_velocity)
    free_velocity = jnp.where(guid_index == 0, other_velocity, own_velocity)
    guided = free_velocity + guide_scale * (cond_velocity - free_velocity)
    step_value = step[0].astype(jnp.float32)
    advanced = latent + (sigma_level(step_value + 1.0) - sigma_level(step_value)) * guided
    return (advanced, guided)


def solution(mesh):
    shape = mesh.devices.shape
    cores = 2
    fine = jax.sharding.Mesh(
        mesh.devices.reshape(shape[0], shape[1] // cores, cores, shape[2]),
        ("guid", "xlo", "core", "seq"),
    )
    req = ("xlo", "core")
    every = ("guid", "xlo", "core", "seq")
    placed = (
        P("guid", req, "seq", None),
        P("guid", req, "seq", None),
        P("guid", req, None, None),
        P("guid", req, None, None),
        P(every, None),
        P(every, None),
        P(every, None),
        P(every, None),
        P("guid", req),
        P(req, "seq", "guid"),
        P(),
    )
    return jax.shard_map(
        local,
        mesh=fine,
        in_specs=placed,
        out_specs=(P(req, "seq", "guid"), P(req, "seq", "guid")),
        check_vma=False,
    )
```

```python
import jax
import jax.numpy as jnp
from jax import lax
from jax.sharding import PartitionSpec as P

HD = 64
STEPS = 28


norm_epsilon = 1e-06
flow_shift = 3.0
guide_scale = 4.5


def partner(value, axis, bit):
    mask = 2**bit
    pairs = [(source, source ^ mask) for source in range(lax.axis_size(axis))]
    return lax.ppermute(value, axis, pairs)


def modulate(values_in, shift_vec, scale_vec):
    values_in = values_in.astype(jnp.float32)
    average = jnp.mean(values_in, axis=-1, keepdims=True)
    variance = jnp.mean((values_in - average) ** 2, axis=-1, keepdims=True)
    normed = (values_in - average) * lax.rsqrt(variance + norm_epsilon)
    return (normed * (1.0 + scale_vec[..., None, :]) + shift_vec[..., None, :]).astype(jnp.bfloat16)


def sigma_level(step_value):
    remaining = 1.0 - step_value / STEPS
    return flow_shift * remaining / (1.0 + (flow_shift - 1.0) * remaining)


def local(
    img_hidden,
    txt_hidden,
    img_mod,
    txt_mod,
    w_img_qkv,
    w_txt_qkv,
    w_out,
    w_head,
    text_lengths,
    latent,
    step,
):
    all_axes = ("guid", "xlo", "core", "seq")
    prompts = img_hidden.shape[1]
    img_rows = img_hidden.shape[2]
    txt_rows = txt_hidden.shape[2]
    model_width = img_hidden.shape[3]
    nseq = lax.axis_size("seq")

    attn_width = w_img_qkv.shape[1] // 3
    full_txt = lax.all_gather(w_txt_qkv[:, attn_width:], all_axes, axis=0, tiled=True)
    full_img = lax.all_gather(w_img_qkv, all_axes, axis=0, tiled=True)
    out_rows, out_cols = w_out.shape
    head_rows, head_cols = w_head.shape
    head_flat = w_head.reshape(1, head_rows * head_cols)
    head_flat = jnp.pad(head_flat, ((0, 0), (0, out_cols - head_rows * head_cols)))
    packed = lax.all_gather(
        jnp.concatenate([w_out, head_flat], axis=0), all_axes, axis=0, tiled=False
    )
    full_out = packed[:, :out_rows].reshape(-1, out_cols)
    full_head = packed[:, out_rows, : head_rows * head_cols].reshape(-1, head_cols)

    image_in = modulate(img_hidden[0], img_mod[0, :, 0], img_mod[0, :, 1])
    text_in = modulate(txt_hidden[0], txt_mod[0, :, 0], txt_mod[0, :, 1])
    head_count = attn_width // HD
    per_dev = head_count // nseq
    qkv_image = jnp.einsum(
        "prd,de->pre", image_in, full_img, preferred_element_type=jnp.float32
    ).astype(jnp.bfloat16)
    qkv_text = jnp.einsum(
        "prd,de->pre", text_in, full_txt, preferred_element_type=jnp.float32
    ).astype(jnp.bfloat16)

    img_split = qkv_image.reshape(prompts, img_rows, 3, nseq, per_dev * HD)
    img_heads = lax.all_to_all(img_split, "seq", 3, 1, tiled=True)
    txt_split = qkv_text.reshape(prompts, txt_rows, 2, nseq, per_dev * HD)
    txt_heads = lax.all_to_all(txt_split, "seq", 3, 1, tiled=True)
    all_img = img_heads.shape[1]
    all_txt = txt_heads.shape[1]

    query_heads = img_heads[:, :, 0, 0].reshape(prompts, all_img, per_dev, HD)
    key_heads = jnp.concatenate(
        [img_heads[:, :, 1, 0], txt_heads[:, :, 0, 0]], axis=1
    ).reshape(prompts, all_img + all_txt, per_dev, HD)
    value_heads = jnp.concatenate(
        [img_heads[:, :, 2, 0], txt_heads[:, :, 1, 0]], axis=1
    ).reshape(prompts, all_img + all_txt, per_dev, HD)

    lengths = text_lengths[0]
    scores = (
        jnp.einsum("pqhd,pkhd->phqk", query_heads, key_heads, preferred_element_type=jnp.float32)
        * 0.125
    )
    position = jnp.arange(all_img + all_txt, dtype=jnp.int32)
    allowed = (position < all_img)[None, :] | ((position - all_img)[None, :] < lengths[:, None])
    scores = jnp.where(allowed[:, None, None, :], scores, -1e30)
    highest = jnp.max(scores, axis=-1)
    weights = jnp.exp(scores - highest[..., None])
    totals = jnp.sum(weights, axis=-1)
    accumulated = jnp.einsum(
        "phqk,pkhd->pqhd",
        weights.astype(jnp.bfloat16),
        value_heads,
        preferred_element_type=jnp.float32,
    )
    mixture = accumulated / jnp.transpose(totals, (0, 2, 1))[..., None]
    head_out = mixture.astype(jnp.bfloat16).reshape(prompts, all_img, 1, per_dev * HD)
    token_out = lax.all_to_all(head_out, "seq", 1, 2, tiled=True)
    attended = token_out.reshape(prompts * img_rows, attn_width)

    projected = jnp.dot(attended, full_out, preferred_element_type=jnp.float32)
    residual = img_hidden[0].astype(jnp.float32) + img_mod[0, :, 2][:, None, :] * projected.reshape(
        prompts, img_rows, model_width
    )
    final_in = modulate(residual, img_mod[0, :, 3], img_mod[0, :, 4])
    guid_index = lax.axis_index("guid")
    half_width = latent.shape[2]
    own_start = guid_index * half_width
    other_start = (1 - guid_index) * half_width
    whole_velocity = jnp.einsum(
        "prd,dc->prc", final_in, full_head, preferred_element_type=jnp.float32
    )
    own_velocity = lax.dynamic_slice_in_dim(whole_velocity, own_start, half_width, 2)
    partner_part = lax.dynamic_slice_in_dim(whole_velocity, other_start, half_width, 2)
    other_velocity = partner(partner_part.astype(jnp.bfloat16), "guid", 0).astype(
        partner_part.dtype
    )
    cond_velocity = jnp.where(guid_index == 0, own_velocity, other_velocity)
    free_velocity = jnp.where(guid_index == 0, other_velocity, own_velocity)
    guided = free_velocity + guide_scale * (cond_velocity - free_velocity)
    step_value = step[0].astype(jnp.float32)
    advanced = latent + (sigma_level(step_value + 1.0) - sigma_level(step_value)) * guided
    return (advanced, guided)


def solution(mesh):
    shape = mesh.devices.shape
    cores = 2
    fine = jax.sharding.Mesh(
        mesh.devices.reshape(shape[0], shape[1] // cores, cores, shape[2]),
        ("guid", "xlo", "core", "seq"),
    )
    req = ("xlo", "core")
    every = ("guid", "xlo", "core", "seq")
    placed = (
        P("guid", req, "seq", None),
        P("guid", req, "seq", None),
        P("guid", req, None, None),
        P("guid", req, None, None),
        P(every, None),
        P(every, None),
        P(every, None),
        P(every, None),
        P("guid", req),
        P(req, "seq", "guid"),
        P(),
    )
    return jax.shard_map(
        local,
        mesh=fine,
        in_specs=placed,
        out_specs=(P(req, "seq", "guid"), P(req, "seq", "guid")),
        check_vma=False,
    )
```

```python
import jax
import jax.numpy as jnp
from jax import lax
from jax.sharding import PartitionSpec as P
from jax.experimental import pallas as pl
from jax.experimental.pallas import tpu as pltpu

HD = 64
STEPS = 28


norm_epsilon = 1e-06
flow_shift = 3.0
guide_scale = 4.5


def partner(value, axis, bit):
    mask = 2**bit
    pairs = [(source, source ^ mask) for source in range(lax.axis_size(axis))]
    return lax.ppermute(value, axis, pairs)


def modulate(values_in, shift_vec, scale_vec):
    values_in = values_in.astype(jnp.float32)
    average = jnp.mean(values_in, axis=-1, keepdims=True)
    variance = jnp.mean((values_in - average) ** 2, axis=-1, keepdims=True)
    normed = (values_in - average) * lax.rsqrt(variance + norm_epsilon)
    return (normed * (1.0 + scale_vec[..., None, :]) + shift_vec[..., None, :]).astype(jnp.bfloat16)


def sigma_level(step_value):
    remaining = 1.0 - step_value / STEPS
    return flow_shift * remaining / (1.0 + (flow_shift - 1.0) * remaining)


def attend_kernel(len_ref, q_ref, ki_ref, vi_ref, kt_ref, vt_ref, o_ref):
    length = len_ref[pl.program_id(0)]
    q = q_ref[0]
    dims = (((1,), (1,)), ((), ()))
    s_img = lax.dot_general(q, ki_ref[0], dims, preferred_element_type=jnp.float32) * 0.125
    s_txt = lax.dot_general(q, kt_ref[0], dims, preferred_element_type=jnp.float32) * 0.125
    col = lax.broadcasted_iota(jnp.int32, s_txt.shape, 1)
    s_txt = jnp.where(col < length, s_txt, -1e30)
    highest = jnp.maximum(
        jnp.max(s_img, axis=1, keepdims=True), jnp.max(s_txt, axis=1, keepdims=True)
    )
    e_img = jnp.exp(s_img - highest)
    e_txt = jnp.exp(s_txt - highest)
    totals = jnp.sum(e_img, axis=1, keepdims=True) + jnp.sum(e_txt, axis=1, keepdims=True)
    acc = jnp.dot(
        e_img.astype(jnp.bfloat16), vi_ref[0], preferred_element_type=jnp.float32
    ) + jnp.dot(e_txt.astype(jnp.bfloat16), vt_ref[0], preferred_element_type=jnp.float32)
    o_ref[0] = (acc / totals).astype(o_ref.dtype)


def attend(lengths, q, k_img, v_img, k_txt, v_txt, block=256):
    batch, rows, width = q.shape
    n_img = k_img.shape[1]
    n_txt = k_txt.shape[1]
    flops = 4 * batch * rows * (n_img + n_txt) * width
    moved = 2 * (q.size * 2 + k_img.size * 2 + k_txt.size * 2)
    return pl.pallas_call(
        attend_kernel,
        grid=(batch, rows // block),
        in_specs=[
            pl.BlockSpec(memory_space=pltpu.SMEM),
            pl.BlockSpec((1, block, width), lambda b, i: (b, i, 0)),
            pl.BlockSpec((1, n_img, width), lambda b, i: (b, 0, 0)),
            pl.BlockSpec((1, n_img, width), lambda b, i: (b, 0, 0)),
            pl.BlockSpec((1, n_txt, width), lambda b, i: (b, 0, 0)),
            pl.BlockSpec((1, n_txt, width), lambda b, i: (b, 0, 0)),
        ],
        out_specs=pl.BlockSpec((1, block, width), lambda b, i: (b, i, 0)),
        out_shape=jax.ShapeDtypeStruct(q.shape, jnp.bfloat16),
        cost_estimate=pl.CostEstimate(
            flops=flops, transcendentals=batch * rows * (n_img + n_txt), bytes_accessed=moved
        ),
    )(lengths, q, k_img, v_img, k_txt, v_txt)


def local(
    img_hidden,
    txt_hidden,
    img_mod,
    txt_mod,
    w_img_qkv,
    w_txt_qkv,
    w_out,
    w_head,
    text_lengths,
    latent,
    step,
):
    all_axes = ("guid", "xlo", "core", "seq")
    prompts = img_hidden.shape[1]
    img_rows = img_hidden.shape[2]
    txt_rows = txt_hidden.shape[2]
    model_width = img_hidden.shape[3]
    nseq = lax.axis_size("seq")

    attn_width = w_img_qkv.shape[1] // 3
    full_txt = lax.all_gather(w_txt_qkv[:, attn_width:], all_axes, axis=0, tiled=True)
    full_img = lax.all_gather(w_img_qkv, all_axes, axis=0, tiled=True)
    out_rows, out_cols = w_out.shape
    head_rows, head_cols = w_head.shape
    head_flat = w_head.reshape(1, head_rows * head_cols)
    head_flat = jnp.pad(head_flat, ((0, 0), (0, out_cols - head_rows * head_cols)))
    packed = lax.all_gather(
        jnp.concatenate([w_out, head_flat], axis=0), all_axes, axis=0, tiled=False
    )
    full_out = packed[:, :out_rows].reshape(-1, out_cols)
    full_head = packed[:, out_rows, : head_rows * head_cols].reshape(-1, head_cols)

    image_in = modulate(img_hidden[0], img_mod[0, :, 0], img_mod[0, :, 1])
    text_in = modulate(txt_hidden[0], txt_mod[0, :, 0], txt_mod[0, :, 1])
    head_count = attn_width // HD
    per_dev = head_count // nseq
    qkv_image = jnp.einsum(
        "prd,de->pre", image_in, full_img, preferred_element_type=jnp.float32
    ).astype(jnp.bfloat16)
    qkv_text = jnp.einsum(
        "prd,de->pre", text_in, full_txt, preferred_element_type=jnp.float32
    ).astype(jnp.bfloat16)

    img_split = qkv_image.reshape(prompts, img_rows, 3, nseq, per_dev * HD)
    img_heads = lax.all_to_all(img_split, "seq", 3, 1, tiled=True)
    txt_split = qkv_text.reshape(prompts, txt_rows, 2, nseq, per_dev * HD)
    txt_heads = lax.all_to_all(txt_split, "seq", 3, 1, tiled=True)
    all_img = img_heads.shape[1]
    all_txt = txt_heads.shape[1]

    assert per_dev == 1
    lengths = text_lengths[0]
    mixture = attend(
        lengths,
        img_heads[:, :, 0, 0],
        img_heads[:, :, 1, 0],
        img_heads[:, :, 2, 0],
        txt_heads[:, :, 0, 0],
        txt_heads[:, :, 1, 0],
    )
    head_out = mixture.reshape(prompts, all_img, 1, per_dev * HD)
    token_out = lax.all_to_all(head_out, "seq", 1, 2, tiled=True)
    attended = token_out.reshape(prompts * img_rows, attn_width)

    projected = jnp.dot(attended, full_out, preferred_element_type=jnp.float32)
    residual = img_hidden[0].astype(jnp.float32) + img_mod[0, :, 2][:, None, :] * projected.reshape(
        prompts, img_rows, model_width
    )
    final_in = modulate(residual, img_mod[0, :, 3], img_mod[0, :, 4])
    guid_index = lax.axis_index("guid")
    half_width = latent.shape[2]
    own_start = guid_index * half_width
    other_start = (1 - guid_index) * half_width
    whole_velocity = jnp.einsum(
        "prd,dc->prc", final_in, full_head, preferred_element_type=jnp.float32
    )
    own_velocity = lax.dynamic_slice_in_dim(whole_velocity, own_start, half_width, 2)
    partner_part = lax.dynamic_slice_in_dim(whole_velocity, other_start, half_width, 2)
    other_velocity = partner(partner_part.astype(jnp.bfloat16), "guid", 0).astype(
        partner_part.dtype
    )
    cond_velocity = jnp.where(guid_index == 0, own_velocity, other_velocity)
    free_velocity = jnp.where(guid_index == 0, other_velocity, own_velocity)
    guided = free_velocity + guide_scale * (cond_velocity - free_velocity)
    step_value = step[0].astype(jnp.float32)
    advanced = latent + (sigma_level(step_value + 1.0) - sigma_level(step_value)) * guided
    return (advanced, guided)


def solution(mesh):
    shape = mesh.devices.shape
    cores = 2
    fine = jax.sharding.Mesh(
        mesh.devices.reshape(shape[0], shape[1] // cores, cores, shape[2]),
        ("guid", "xlo", "core", "seq"),
    )
    req = ("xlo", "core")
    every = ("guid", "xlo", "core", "seq")
    placed = (
        P("guid", req, "seq", None),
        P("guid", req, "seq", None),
        P("guid", req, None, None),
        P("guid", req, None, None),
        P(every, None),
        P(every, None),
        P(every, None),
        P(every, None),
        P("guid", req),
        P(req, "seq", "guid"),
        P(),
    )
    return jax.shard_map(
        local,
        mesh=fine,
        in_specs=placed,
        out_specs=(P(req, "seq", "guid"), P(req, "seq", "guid")),
        check_vma=False,
    )
```

```python
import jax
import jax.numpy as jnp
from jax import lax
from jax.sharding import PartitionSpec as P
from jax.experimental import pallas as pl
from jax.experimental.pallas import tpu as pltpu

HD = 64
STEPS = 28


norm_epsilon = 1e-06
flow_shift = 3.0
guide_scale = 4.5


def partner(value, axis, bit):
    mask = 2**bit
    pairs = [(source, source ^ mask) for source in range(lax.axis_size(axis))]
    return lax.ppermute(value, axis, pairs)


def modulate(values_in, shift_vec, scale_vec):
    values_in = values_in.astype(jnp.float32)
    average = jnp.mean(values_in, axis=-1, keepdims=True)
    variance = jnp.mean((values_in - average) ** 2, axis=-1, keepdims=True)
    normed = (values_in - average) * lax.rsqrt(variance + norm_epsilon)
    return (normed * (1.0 + scale_vec[..., None, :]) + shift_vec[..., None, :]).astype(jnp.bfloat16)


def sigma_level(step_value):
    remaining = 1.0 - step_value / STEPS
    return flow_shift * remaining / (1.0 + (flow_shift - 1.0) * remaining)


def attend_kernel(len_ref, q_ref, ki_ref, vi_ref, kt_ref, vt_ref, o_ref):
    length = len_ref[pl.program_id(0)]
    q = q_ref[0]
    dims = (((1,), (1,)), ((), ()))
    s_img = lax.dot_general(q, ki_ref[0], dims, preferred_element_type=jnp.float32) * 0.125
    s_txt = lax.dot_general(q, kt_ref[0], dims, preferred_element_type=jnp.float32) * 0.125
    col = lax.broadcasted_iota(jnp.int32, s_txt.shape, 1)
    s_txt = jnp.where(col < length, s_txt, -1e30)
    highest = jnp.maximum(
        jnp.max(s_img, axis=1, keepdims=True), jnp.max(s_txt, axis=1, keepdims=True)
    )
    e_img = jnp.exp(s_img - highest)
    e_txt = jnp.exp(s_txt - highest)
    totals = jnp.sum(e_img, axis=1, keepdims=True) + jnp.sum(e_txt, axis=1, keepdims=True)
    acc = jnp.dot(
        e_img.astype(jnp.bfloat16), vi_ref[0], preferred_element_type=jnp.float32
    ) + jnp.dot(e_txt.astype(jnp.bfloat16), vt_ref[0], preferred_element_type=jnp.float32)
    o_ref[0] = (acc / totals).astype(o_ref.dtype)


def attend(lengths, q, k_img, v_img, k_txt, v_txt, block=256):
    batch, rows, width = q.shape
    n_img = k_img.shape[1]
    n_txt = k_txt.shape[1]
    flops = 4 * batch * rows * (n_img + n_txt) * width
    moved = 2 * (q.size * 2 + k_img.size * 2 + k_txt.size * 2)
    return pl.pallas_call(
        attend_kernel,
        grid=(batch, rows // block),
        in_specs=[
            pl.BlockSpec(memory_space=pltpu.SMEM),
            pl.BlockSpec((1, block, width), lambda b, i: (b, i, 0)),
            pl.BlockSpec((1, n_img, width), lambda b, i: (b, 0, 0)),
            pl.BlockSpec((1, n_img, width), lambda b, i: (b, 0, 0)),
            pl.BlockSpec((1, n_txt, width), lambda b, i: (b, 0, 0)),
            pl.BlockSpec((1, n_txt, width), lambda b, i: (b, 0, 0)),
        ],
        out_specs=pl.BlockSpec((1, block, width), lambda b, i: (b, i, 0)),
        out_shape=jax.ShapeDtypeStruct(q.shape, jnp.bfloat16),
        cost_estimate=pl.CostEstimate(
            flops=flops, transcendentals=batch * rows * (n_img + n_txt), bytes_accessed=moved
        ),
    )(lengths, q, k_img, v_img, k_txt, v_txt)


def block(
    img_hidden,
    txt_hidden,
    img_mod,
    txt_mod,
    w_img_qkv,
    w_txt_qkv,
    w_out,
    w_head,
    text_lengths,
    latent,
    step,
):
    all_axes = ("guid", "xlo", "core", "seq")
    prompts = img_hidden.shape[1]
    img_rows = img_hidden.shape[2]
    txt_rows = txt_hidden.shape[2]
    model_width = img_hidden.shape[3]
    nseq = lax.axis_size("seq")

    attn_width = w_img_qkv.shape[1] // 3
    img_kv_rows = w_img_qkv[:, attn_width:]
    img_q_rows = w_img_qkv[:, :attn_width]
    txt_kv_rows = w_txt_qkv[:, attn_width:]
    full_img_kv = lax.all_gather(img_kv_rows, all_axes, axis=0, tiled=True)
    full_img_q = lax.all_gather(img_q_rows, all_axes, axis=0, tiled=True)
    full_txt = lax.all_gather(txt_kv_rows, all_axes, axis=0, tiled=True)
    out_rows, out_cols = w_out.shape
    head_rows, head_cols = w_head.shape
    head_flat = w_head.reshape(1, head_rows * head_cols)
    head_flat = jnp.pad(head_flat, ((0, 0), (0, out_cols - head_rows * head_cols)))
    out_rows_local = jnp.concatenate([w_out, head_flat], axis=0)
    packed = lax.all_gather(out_rows_local, all_axes, axis=0, tiled=False)
    full_out = packed[:, :out_rows].reshape(-1, out_cols)
    full_head = packed[:, out_rows, : head_rows * head_cols].reshape(-1, head_cols)

    image_in = modulate(img_hidden[0], img_mod[0, :, 0], img_mod[0, :, 1])
    text_in = modulate(txt_hidden[0], txt_mod[0, :, 0], txt_mod[0, :, 1])
    head_count = attn_width // HD
    per_dev = head_count // nseq
    kv_image = jnp.einsum(
        "prd,de->pre", image_in, full_img_kv, preferred_element_type=jnp.float32
    ).astype(jnp.bfloat16)
    q_image = jnp.einsum(
        "prd,de->pre", image_in, full_img_q, preferred_element_type=jnp.float32
    ).astype(jnp.bfloat16)
    qkv_text = jnp.einsum(
        "prd,de->pre", text_in, full_txt, preferred_element_type=jnp.float32
    ).astype(jnp.bfloat16)

    kv_heads = lax.all_to_all(
        kv_image.reshape(prompts, img_rows, 2, nseq, per_dev * HD), "seq", 3, 1, tiled=True
    )
    q_heads = lax.all_to_all(
        q_image.reshape(prompts, img_rows, nseq, per_dev * HD), "seq", 2, 1, tiled=True
    )
    txt_heads = lax.all_to_all(
        qkv_text.reshape(prompts, txt_rows, 2, nseq, per_dev * HD), "seq", 3, 1, tiled=True
    )
    all_img = q_heads.shape[1]

    assert per_dev == 1
    lengths = text_lengths[0]
    mixture = attend(
        lengths,
        q_heads[:, :, 0],
        kv_heads[:, :, 0, 0],
        kv_heads[:, :, 1, 0],
        txt_heads[:, :, 0, 0],
        txt_heads[:, :, 1, 0],
    )
    head_out = mixture.reshape(prompts, all_img, 1, per_dev * HD)
    token_out = lax.all_to_all(head_out, "seq", 1, 2, tiled=True)
    attended = token_out.reshape(prompts * img_rows, attn_width)

    projected = jnp.dot(attended, full_out, preferred_element_type=jnp.float32)
    residual = img_hidden[0].astype(jnp.float32) + img_mod[0, :, 2][:, None, :] * projected.reshape(
        prompts, img_rows, model_width
    )
    final_in = modulate(residual, img_mod[0, :, 3], img_mod[0, :, 4])
    guid_index = lax.axis_index("guid")
    half_width = latent.shape[2]
    own_start = guid_index * half_width
    other_start = (1 - guid_index) * half_width
    whole_velocity = jnp.einsum(
        "prd,dc->prc", final_in, full_head, preferred_element_type=jnp.float32
    )
    own_velocity = lax.dynamic_slice_in_dim(whole_velocity, own_start, half_width, 2)
    partner_part = lax.dynamic_slice_in_dim(whole_velocity, other_start, half_width, 2)
    other_velocity = partner(partner_part.astype(jnp.bfloat16), "guid", 0).astype(
        partner_part.dtype
    )
    cond_velocity = jnp.where(guid_index == 0, own_velocity, other_velocity)
    free_velocity = jnp.where(guid_index == 0, other_velocity, own_velocity)
    guided = free_velocity + guide_scale * (cond_velocity - free_velocity)
    step_value = step[0].astype(jnp.float32)
    advanced = latent + (sigma_level(step_value + 1.0) - sigma_level(step_value)) * guided
    return (advanced, guided)


def solution(mesh):
    shape = mesh.devices.shape
    cores = 2
    fine = jax.sharding.Mesh(
        mesh.devices.reshape(shape[0], shape[1] // cores, cores, shape[2]),
        ("guid", "xlo", "core", "seq"),
    )
    req = ("xlo", "core")
    every = ("guid", "xlo", "core", "seq")
    placed = (
        P("guid", req, "seq", None),
        P("guid", req, "seq", None),
        P("guid", req, None, None),
        P("guid", req, None, None),
        P(every, None),
        P(every, None),
        P(every, None),
        P(every, None),
        P("guid", req),
        P(req, "seq", "guid"),
        P(),
    )
    return jax.shard_map(
        block,
        mesh=fine,
        in_specs=placed,
        out_specs=(P(req, "seq", "guid"), P(req, "seq", "guid")),
        check_vma=False,
    )
```

```python
import jax
import jax.numpy as jnp
from jax import lax
from jax.sharding import PartitionSpec as P
from jax.experimental import pallas as pl
from jax.experimental.pallas import tpu as pltpu

HD = 64
STEPS = 28


norm_epsilon = 1e-06
flow_shift = 3.0
guide_scale = 4.5


def partner(value, axis, bit):
    mask = 2**bit
    pairs = [(source, source ^ mask) for source in range(lax.axis_size(axis))]
    return lax.ppermute(value, axis, pairs)


def modulate(values_in, shift_vec, scale_vec):
    values_in = values_in.astype(jnp.float32)
    average = jnp.mean(values_in, axis=-1, keepdims=True)
    variance = jnp.mean((values_in - average) ** 2, axis=-1, keepdims=True)
    normed = (values_in - average) * lax.rsqrt(variance + norm_epsilon)
    return (normed * (1.0 + scale_vec[..., None, :]) + shift_vec[..., None, :]).astype(jnp.bfloat16)


def sigma_level(step_value):
    remaining = 1.0 - step_value / STEPS
    return flow_shift * remaining / (1.0 + (flow_shift - 1.0) * remaining)


def attend_kernel(len_ref, q_ref, ki_ref, vi_ref, kt_ref, vt_ref, o_ref):
    length = len_ref[pl.program_id(0)]
    q = q_ref[0]
    dims = (((1,), (1,)), ((), ()))
    s_img = lax.dot_general(q, ki_ref[0], dims, preferred_element_type=jnp.float32) * 0.125
    s_txt = lax.dot_general(q, kt_ref[0], dims, preferred_element_type=jnp.float32) * 0.125
    col = lax.broadcasted_iota(jnp.int32, s_txt.shape, 1)
    s_txt = jnp.where(col < length, s_txt, -1e30)
    highest = jnp.maximum(
        jnp.max(s_img, axis=1, keepdims=True), jnp.max(s_txt, axis=1, keepdims=True)
    )
    e_img = jnp.exp(s_img - highest)
    e_txt = jnp.exp(s_txt - highest)
    totals = jnp.sum(e_img, axis=1, keepdims=True) + jnp.sum(e_txt, axis=1, keepdims=True)
    acc = jnp.dot(
        e_img.astype(jnp.bfloat16), vi_ref[0], preferred_element_type=jnp.float32
    ) + jnp.dot(e_txt.astype(jnp.bfloat16), vt_ref[0], preferred_element_type=jnp.float32)
    o_ref[0] = (acc / totals).astype(o_ref.dtype)


def attend(lengths, q, k_img, v_img, k_txt, v_txt, block=256):
    batch, rows, width = q.shape
    n_img = k_img.shape[1]
    n_txt = k_txt.shape[1]
    flops = 4 * batch * rows * (n_img + n_txt) * width
    moved = 2 * (q.size * 2 + k_img.size * 2 + k_txt.size * 2)
    return pl.pallas_call(
        attend_kernel,
        grid=(batch, rows // block),
        in_specs=[
            pl.BlockSpec(memory_space=pltpu.SMEM),
            pl.BlockSpec((1, block, width), lambda b, i: (b, i, 0)),
            pl.BlockSpec((1, n_img, width), lambda b, i: (b, 0, 0)),
            pl.BlockSpec((1, n_img, width), lambda b, i: (b, 0, 0)),
            pl.BlockSpec((1, n_txt, width), lambda b, i: (b, 0, 0)),
            pl.BlockSpec((1, n_txt, width), lambda b, i: (b, 0, 0)),
        ],
        out_specs=pl.BlockSpec((1, block, width), lambda b, i: (b, i, 0)),
        out_shape=jax.ShapeDtypeStruct(q.shape, jnp.bfloat16),
        cost_estimate=pl.CostEstimate(
            flops=flops, transcendentals=batch * rows * (n_img + n_txt), bytes_accessed=moved
        ),
    )(lengths, q, k_img, v_img, k_txt, v_txt)


def local(
    img_hidden,
    txt_hidden,
    img_mod,
    txt_mod,
    w_img_qkv,
    w_txt_qkv,
    w_out,
    w_head,
    text_lengths,
    latent,
    step,
):
    all_axes = ("guid", "xlo", "core", "seq")
    prompts = img_hidden.shape[1]
    img_rows = img_hidden.shape[2]
    txt_rows = txt_hidden.shape[2]
    model_width = img_hidden.shape[3]
    nseq = lax.axis_size("seq")

    attn_width = w_img_qkv.shape[1] // 3
    out_rows, out_cols = w_out.shape
    head_rows, head_cols = w_head.shape
    local_rows = w_img_qkv.shape[0]
    head_flat = w_head.reshape(1, head_rows * head_cols)
    head_flat = jnp.pad(head_flat, ((0, 0), (0, out_cols - head_rows * head_cols)))
    tail = jnp.concatenate([w_out, head_flat], axis=0)
    tail_width = tail.size // local_rows
    img_width = w_img_qkv.shape[1]
    txt_width = w_txt_qkv.shape[1] - attn_width
    local_all = jnp.concatenate(
        [w_img_qkv, w_txt_qkv[:, attn_width:], tail.reshape(local_rows, tail_width)], axis=1
    )
    gathered = lax.all_gather(local_all, all_axes, axis=0, tiled=False)
    full_img = gathered[:, :, :img_width].reshape(-1, img_width)
    full_txt = gathered[:, :, img_width : img_width + txt_width].reshape(-1, txt_width)
    packed = gathered[:, :, img_width + txt_width :].reshape(-1, out_rows + 1, out_cols)
    full_out = packed[:, :out_rows].reshape(-1, out_cols)
    full_head = packed[:, out_rows, : head_rows * head_cols].reshape(-1, head_cols)

    image_in = modulate(img_hidden[0], img_mod[0, :, 0], img_mod[0, :, 1])
    text_in = modulate(txt_hidden[0], txt_mod[0, :, 0], txt_mod[0, :, 1])
    head_count = attn_width // HD
    per_dev = head_count // nseq
    qkv_image = jnp.einsum(
        "prd,de->pre", image_in, full_img, preferred_element_type=jnp.float32
    ).astype(jnp.bfloat16)
    qkv_text = jnp.einsum(
        "prd,de->pre", text_in, full_txt, preferred_element_type=jnp.float32
    ).astype(jnp.bfloat16)

    img_split = qkv_image.reshape(prompts, img_rows, 3, nseq, per_dev * HD)
    img_heads = lax.all_to_all(img_split, "seq", 3, 1, tiled=True)
    txt_split = qkv_text.reshape(prompts, txt_rows, 2, nseq, per_dev * HD)
    txt_heads = lax.all_to_all(txt_split, "seq", 3, 1, tiled=True)
    all_img = img_heads.shape[1]
    all_txt = txt_heads.shape[1]

    assert per_dev == 1
    lengths = text_lengths[0]
    mixture = attend(
        lengths,
        img_heads[:, :, 0, 0],
        img_heads[:, :, 1, 0],
        img_heads[:, :, 2, 0],
        txt_heads[:, :, 0, 0],
        txt_heads[:, :, 1, 0],
    )
    head_out = mixture.reshape(prompts, all_img, 1, per_dev * HD)
    token_out = lax.all_to_all(head_out, "seq", 1, 2, tiled=True)
    attended = token_out.reshape(prompts * img_rows, attn_width)

    projected = jnp.dot(attended, full_out, preferred_element_type=jnp.float32)
    residual = img_hidden[0].astype(jnp.float32) + img_mod[0, :, 2][:, None, :] * projected.reshape(
        prompts, img_rows, model_width
    )
    final_in = modulate(residual, img_mod[0, :, 3], img_mod[0, :, 4])
    guid_index = lax.axis_index("guid")
    half_width = latent.shape[2]
    own_start = guid_index * half_width
    other_start = (1 - guid_index) * half_width
    whole_velocity = jnp.einsum(
        "prd,dc->prc", final_in, full_head, preferred_element_type=jnp.float32
    )
    own_velocity = lax.dynamic_slice_in_dim(whole_velocity, own_start, half_width, 2)
    partner_part = lax.dynamic_slice_in_dim(whole_velocity, other_start, half_width, 2)
    other_velocity = partner(partner_part.astype(jnp.bfloat16), "guid", 0).astype(
        partner_part.dtype
    )
    cond_velocity = jnp.where(guid_index == 0, own_velocity, other_velocity)
    free_velocity = jnp.where(guid_index == 0, other_velocity, own_velocity)
    guided = free_velocity + guide_scale * (cond_velocity - free_velocity)
    step_value = step[0].astype(jnp.float32)
    advanced = latent + (sigma_level(step_value + 1.0) - sigma_level(step_value)) * guided
    return (advanced, guided)


def solution(mesh):
    shape = mesh.devices.shape
    cores = 2
    fine = jax.sharding.Mesh(
        mesh.devices.reshape(shape[0], shape[1] // cores, cores, shape[2]),
        ("guid", "xlo", "core", "seq"),
    )
    req = ("xlo", "core")
    every = ("guid", "xlo", "core", "seq")
    placed = (
        P("guid", req, "seq", None),
        P("guid", req, "seq", None),
        P("guid", req, None, None),
        P("guid", req, None, None),
        P(every, None),
        P(every, None),
        P(every, None),
        P(every, None),
        P("guid", req),
        P(req, "seq", "guid"),
        P(),
    )
    return jax.shard_map(
        local,
        mesh=fine,
        in_specs=placed,
        out_specs=(P(req, "seq", "guid"), P(req, "seq", "guid")),
        check_vma=False,
    )
```

```python
import jax
import jax.numpy as jnp
from jax import lax
from jax.sharding import PartitionSpec as P
from jax.experimental import pallas as pl
from jax.experimental.pallas import tpu as pltpu

HD = 64
STEPS = 28


norm_epsilon = 1e-06
flow_shift = 3.0
guide_scale = 4.5


def partner(value, axis, bit):
    mask = 2**bit
    pairs = [(source, source ^ mask) for source in range(lax.axis_size(axis))]
    return lax.ppermute(value, axis, pairs)


def modulate(values_in, shift_vec, scale_vec):
    values_in = values_in.astype(jnp.float32)
    average = jnp.mean(values_in, axis=-1, keepdims=True)
    variance = jnp.mean((values_in - average) ** 2, axis=-1, keepdims=True)
    normed = (values_in - average) * lax.rsqrt(variance + norm_epsilon)
    return (normed * (1.0 + scale_vec[..., None, :]) + shift_vec[..., None, :]).astype(jnp.bfloat16)


def sigma_level(step_value):
    remaining = 1.0 - step_value / STEPS
    return flow_shift * remaining / (1.0 + (flow_shift - 1.0) * remaining)


def attend_kernel(len_ref, q_ref, ki_ref, vi_ref, kt_ref, vt_ref, o_ref):
    length = len_ref[pl.program_id(0)]
    q = q_ref[0]
    dims = (((1,), (1,)), ((), ()))
    s_img = lax.dot_general(q, ki_ref[0], dims, preferred_element_type=jnp.float32) * 0.125
    s_txt = lax.dot_general(q, kt_ref[0], dims, preferred_element_type=jnp.float32) * 0.125
    col = lax.broadcasted_iota(jnp.int32, s_txt.shape, 1)
    s_txt = jnp.where(col < length, s_txt, -1e30)
    highest = jnp.maximum(
        jnp.max(s_img, axis=1, keepdims=True), jnp.max(s_txt, axis=1, keepdims=True)
    )
    e_img = jnp.exp(s_img - highest)
    e_txt = jnp.exp(s_txt - highest)
    totals = jnp.sum(e_img, axis=1, keepdims=True) + jnp.sum(e_txt, axis=1, keepdims=True)
    acc = jnp.dot(
        e_img.astype(jnp.bfloat16), vi_ref[0], preferred_element_type=jnp.float32
    ) + jnp.dot(e_txt.astype(jnp.bfloat16), vt_ref[0], preferred_element_type=jnp.float32)
    o_ref[0] = (acc / totals).astype(o_ref.dtype)


def attend(lengths, q, k_img, v_img, k_txt, v_txt, block=256):
    batch, rows, width = q.shape
    n_img = k_img.shape[1]
    n_txt = k_txt.shape[1]
    flops = 4 * batch * rows * (n_img + n_txt) * width
    moved = 2 * (q.size * 2 + k_img.size * 2 + k_txt.size * 2)
    return pl.pallas_call(
        attend_kernel,
        grid=(batch, rows // block),
        in_specs=[
            pl.BlockSpec(memory_space=pltpu.SMEM),
            pl.BlockSpec((1, block, width), lambda b, i: (b, i, 0)),
            pl.BlockSpec((1, n_img, width), lambda b, i: (b, 0, 0)),
            pl.BlockSpec((1, n_img, width), lambda b, i: (b, 0, 0)),
            pl.BlockSpec((1, n_txt, width), lambda b, i: (b, 0, 0)),
            pl.BlockSpec((1, n_txt, width), lambda b, i: (b, 0, 0)),
        ],
        out_specs=pl.BlockSpec((1, block, width), lambda b, i: (b, i, 0)),
        out_shape=jax.ShapeDtypeStruct(q.shape, jnp.bfloat16),
        cost_estimate=pl.CostEstimate(
            flops=flops, transcendentals=batch * rows * (n_img + n_txt), bytes_accessed=moved
        ),
    )(lengths, q, k_img, v_img, k_txt, v_txt)


def local(
    img_hidden,
    txt_hidden,
    img_mod,
    txt_mod,
    w_img_qkv,
    w_txt_qkv,
    w_out,
    w_head,
    text_lengths,
    latent,
    step,
):
    all_axes = ("guid", "xlo", "core", "seq")
    prompts = img_hidden.shape[1]
    img_rows = img_hidden.shape[2]
    txt_rows = txt_hidden.shape[2]
    model_width = img_hidden.shape[3]
    nseq = lax.axis_size("seq")

    attn_width = w_img_qkv.shape[1] // 3
    out_rows, out_cols = w_out.shape
    head_rows, head_cols = w_head.shape
    local_rows = w_img_qkv.shape[0]
    head_flat = w_head.reshape(1, head_rows * head_cols)
    head_flat = jnp.pad(head_flat, ((0, 0), (0, out_cols - head_rows * head_cols)))
    tail = jnp.concatenate([w_out, head_flat], axis=0)
    tail_width = tail.size // local_rows
    img_width = w_img_qkv.shape[1]
    txt_width = w_txt_qkv.shape[1] - attn_width
    local_all = jnp.concatenate(
        [w_img_qkv, w_txt_qkv[:, attn_width:], tail.reshape(local_rows, tail_width)], axis=1
    )
    gathered = lax.all_gather(local_all, all_axes, axis=0, tiled=False)
    full_all = gathered.reshape(-1, local_all.shape[1])
    full_img = full_all[:, :img_width]
    full_txt = full_all[:, img_width : img_width + txt_width]
    packed = full_all[:, img_width + txt_width :].reshape(-1, out_rows + 1, out_cols)
    full_out = packed[:, :out_rows].reshape(-1, out_cols)
    full_head = packed[:, out_rows, : head_rows * head_cols].reshape(-1, head_cols)

    image_in = modulate(img_hidden[0], img_mod[0, :, 0], img_mod[0, :, 1])
    text_in = modulate(txt_hidden[0], txt_mod[0, :, 0], txt_mod[0, :, 1])
    head_count = attn_width // HD
    per_dev = head_count // nseq
    qkv_image = jnp.einsum(
        "prd,de->pre", image_in, full_img, preferred_element_type=jnp.float32
    ).astype(jnp.bfloat16)
    qkv_text = jnp.einsum(
        "prd,de->pre", text_in, full_txt, preferred_element_type=jnp.float32
    ).astype(jnp.bfloat16)

    img_split = qkv_image.reshape(prompts, img_rows, 3, nseq, per_dev * HD)
    img_heads = lax.all_to_all(img_split, "seq", 3, 1, tiled=True)
    txt_split = qkv_text.reshape(prompts, txt_rows, 2, nseq, per_dev * HD)
    txt_heads = lax.all_to_all(txt_split, "seq", 3, 1, tiled=True)
    all_img = img_heads.shape[1]
    all_txt = txt_heads.shape[1]

    assert per_dev == 1
    lengths = text_lengths[0]
    mixture = attend(
        lengths,
        img_heads[:, :, 0, 0],
        img_heads[:, :, 1, 0],
        img_heads[:, :, 2, 0],
        txt_heads[:, :, 0, 0],
        txt_heads[:, :, 1, 0],
    )
    head_out = mixture.reshape(prompts, all_img, 1, per_dev * HD)
    token_out = lax.all_to_all(head_out, "seq", 1, 2, tiled=True)
    attended = token_out.reshape(prompts * img_rows, attn_width)

    projected = jnp.dot(attended, full_out, preferred_element_type=jnp.float32)
    residual = img_hidden[0].astype(jnp.float32) + img_mod[0, :, 2][:, None, :] * projected.reshape(
        prompts, img_rows, model_width
    )
    final_in = modulate(residual, img_mod[0, :, 3], img_mod[0, :, 4])
    guid_index = lax.axis_index("guid")
    half_width = latent.shape[2]
    own_start = guid_index * half_width
    other_start = (1 - guid_index) * half_width
    whole_velocity = jnp.einsum(
        "prd,dc->prc", final_in, full_head, preferred_element_type=jnp.float32
    )
    own_velocity = lax.dynamic_slice_in_dim(whole_velocity, own_start, half_width, 2)
    partner_part = lax.dynamic_slice_in_dim(whole_velocity, other_start, half_width, 2)
    other_velocity = partner(partner_part.astype(jnp.bfloat16), "guid", 0).astype(
        partner_part.dtype
    )
    cond_velocity = jnp.where(guid_index == 0, own_velocity, other_velocity)
    free_velocity = jnp.where(guid_index == 0, other_velocity, own_velocity)
    guided = free_velocity + guide_scale * (cond_velocity - free_velocity)
    step_value = step[0].astype(jnp.float32)
    advanced = latent + (sigma_level(step_value + 1.0) - sigma_level(step_value)) * guided
    return (advanced, guided)


def solution(mesh):
    shape = mesh.devices.shape
    cores = 2
    fine = jax.sharding.Mesh(
        mesh.devices.reshape(shape[0], shape[1] // cores, cores, shape[2]),
        ("guid", "xlo", "core", "seq"),
    )
    req = ("xlo", "core")
    every = ("guid", "xlo", "core", "seq")
    placed = (
        P("guid", req, "seq", None),
        P("guid", req, "seq", None),
        P("guid", req, None, None),
        P("guid", req, None, None),
        P(every, None),
        P(every, None),
        P(every, None),
        P(every, None),
        P("guid", req),
        P(req, "seq", "guid"),
        P(),
    )
    return jax.shard_map(
        local,
        mesh=fine,
        in_specs=placed,
        out_specs=(P(req, "seq", "guid"), P(req, "seq", "guid")),
        check_vma=False,
    )
```

```python
import jax
import jax.numpy as jnp
from jax import lax
from jax.sharding import PartitionSpec as P
from jax.experimental import pallas as pl
from jax.experimental.pallas import tpu as pltpu

HD = 64
STEPS = 28


norm_epsilon = 1e-06
flow_shift = 3.0
guide_scale = 4.5


def partner(value, axis, bit):
    mask = 2**bit
    pairs = [(source, source ^ mask) for source in range(lax.axis_size(axis))]
    return lax.ppermute(value, axis, pairs)


def modulate(values_in, shift_vec, scale_vec):
    values_in = values_in.astype(jnp.float32)
    average = jnp.mean(values_in, axis=-1, keepdims=True)
    variance = jnp.mean((values_in - average) ** 2, axis=-1, keepdims=True)
    normed = (values_in - average) * lax.rsqrt(variance + norm_epsilon)
    return (normed * (1.0 + scale_vec[..., None, :]) + shift_vec[..., None, :]).astype(jnp.bfloat16)


def sigma_level(step_value):
    remaining = 1.0 - step_value / STEPS
    return flow_shift * remaining / (1.0 + (flow_shift - 1.0) * remaining)


def attend_kernel(len_ref, q_ref, ki_ref, vi_ref, kt_ref, vt_ref, o_ref):
    length = len_ref[pl.program_id(0)]
    q = q_ref[0]
    dims = (((1,), (1,)), ((), ()))
    s_img = lax.dot_general(q, ki_ref[0], dims, preferred_element_type=jnp.float32) * 0.125
    s_txt = lax.dot_general(q, kt_ref[0], dims, preferred_element_type=jnp.float32) * 0.125
    col = lax.broadcasted_iota(jnp.int32, s_txt.shape, 1)
    s_txt = jnp.where(col < length, s_txt, -1e30)
    highest = jnp.maximum(
        jnp.max(s_img, axis=1, keepdims=True), jnp.max(s_txt, axis=1, keepdims=True)
    )
    e_img = jnp.exp(s_img - highest)
    e_txt = jnp.exp(s_txt - highest)
    totals = jnp.sum(e_img, axis=1, keepdims=True) + jnp.sum(e_txt, axis=1, keepdims=True)
    acc = jnp.dot(
        e_img.astype(jnp.bfloat16), vi_ref[0], preferred_element_type=jnp.float32
    ) + jnp.dot(e_txt.astype(jnp.bfloat16), vt_ref[0], preferred_element_type=jnp.float32)
    o_ref[0] = (acc / totals).astype(o_ref.dtype)


def attend(lengths, q, k_img, v_img, k_txt, v_txt, block=256):
    batch, rows, width = q.shape
    n_img = k_img.shape[1]
    n_txt = k_txt.shape[1]
    flops = 4 * batch * rows * (n_img + n_txt) * width
    moved = 2 * (q.size * 2 + k_img.size * 2 + k_txt.size * 2)
    return pl.pallas_call(
        attend_kernel,
        grid=(batch, rows // block),
        in_specs=[
            pl.BlockSpec(memory_space=pltpu.SMEM),
            pl.BlockSpec((1, block, width), lambda b, i: (b, i, 0)),
            pl.BlockSpec((1, n_img, width), lambda b, i: (b, 0, 0)),
            pl.BlockSpec((1, n_img, width), lambda b, i: (b, 0, 0)),
            pl.BlockSpec((1, n_txt, width), lambda b, i: (b, 0, 0)),
            pl.BlockSpec((1, n_txt, width), lambda b, i: (b, 0, 0)),
        ],
        out_specs=pl.BlockSpec((1, block, width), lambda b, i: (b, i, 0)),
        out_shape=jax.ShapeDtypeStruct(q.shape, jnp.bfloat16),
        cost_estimate=pl.CostEstimate(
            flops=flops, transcendentals=batch * rows * (n_img + n_txt), bytes_accessed=moved
        ),
    )(lengths, q, k_img, v_img, k_txt, v_txt)


def local(
    img_hidden,
    txt_hidden,
    img_mod,
    txt_mod,
    w_img_qkv,
    w_txt_qkv,
    w_out,
    w_head,
    text_lengths,
    latent,
    step,
):
    all_axes = ("guid", "xlo", "core", "seq")
    prompts = img_hidden.shape[1]
    img_rows = img_hidden.shape[2]
    txt_rows = txt_hidden.shape[2]
    model_width = img_hidden.shape[3]
    nseq = lax.axis_size("seq")

    attn_width = w_img_qkv.shape[1] // 3
    out_rows, out_cols = w_out.shape
    head_rows, head_cols = w_head.shape
    local_rows = w_img_qkv.shape[0]
    head_flat = w_head.reshape(1, head_rows * head_cols)
    head_flat = jnp.pad(head_flat, ((0, 0), (0, out_cols - head_rows * head_cols)))
    tail = jnp.concatenate([w_out, head_flat], axis=0)
    tail_width = tail.size // local_rows
    img_width = w_img_qkv.shape[1]
    txt_width = w_txt_qkv.shape[1] - attn_width
    local_all = jnp.concatenate(
        [w_img_qkv, w_txt_qkv[:, attn_width:], tail.reshape(local_rows, tail_width)], axis=1
    )
    gathered = lax.all_gather(local_all, all_axes, axis=0, tiled=False)
    full_all = gathered.reshape(-1, local_all.shape[1])
    full_img = full_all[:, :img_width]
    full_txt = full_all[:, img_width : img_width + txt_width]
    packed = full_all[:, img_width + txt_width :].reshape(-1, out_rows + 1, out_cols)
    full_out = packed[:, :out_rows].reshape(-1, out_cols)
    full_head = packed[:, out_rows, : head_rows * head_cols].reshape(-1, head_cols)

    image_in = modulate(img_hidden[0], img_mod[0, :, 0], img_mod[0, :, 1])
    text_in = modulate(txt_hidden[0], txt_mod[0, :, 0], txt_mod[0, :, 1])
    head_count = attn_width // HD
    per_dev = head_count // nseq
    qkv_image = jnp.einsum(
        "prd,de->pre", image_in, full_img, preferred_element_type=jnp.float32
    ).astype(jnp.bfloat16)
    qkv_text = jnp.einsum(
        "prd,de->pre", text_in, full_txt, preferred_element_type=jnp.float32
    ).astype(jnp.bfloat16)

    width = per_dev * HD
    img_send = jnp.transpose(
        qkv_image.reshape(prompts, img_rows, 3, nseq, width), (3, 0, 1, 2, 4)
    ).reshape(nseq, -1)
    txt_send = jnp.transpose(
        qkv_text.reshape(prompts, txt_rows, 2, nseq, width), (3, 0, 1, 2, 4)
    ).reshape(nseq, -1)
    n_img = img_send.shape[1]
    received = lax.all_to_all(
        jnp.concatenate([img_send, txt_send], axis=1), "seq", 0, 0, tiled=True
    )
    img_recv = received[:, :n_img].reshape(nseq, prompts, img_rows, 3, width)
    txt_recv = received[:, n_img:].reshape(nseq, prompts, txt_rows, 2, width)

    def rows_of(part, which):
        picked = part[:, :, :, which]
        return jnp.transpose(picked, (1, 0, 2, 3)).reshape(prompts, -1, width)

    all_img = nseq * img_rows
    assert per_dev == 1
    lengths = text_lengths[0]
    mixture = attend(
        lengths,
        rows_of(img_recv, 0),
        rows_of(img_recv, 1),
        rows_of(img_recv, 2),
        rows_of(txt_recv, 0),
        rows_of(txt_recv, 1),
    )
    head_out = mixture.reshape(prompts, all_img, 1, per_dev * HD)
    token_out = lax.all_to_all(head_out, "seq", 1, 2, tiled=True)
    attended = token_out.reshape(prompts * img_rows, attn_width)

    projected = jnp.dot(attended, full_out, preferred_element_type=jnp.float32)
    residual = img_hidden[0].astype(jnp.float32) + img_mod[0, :, 2][:, None, :] * projected.reshape(
        prompts, img_rows, model_width
    )
    final_in = modulate(residual, img_mod[0, :, 3], img_mod[0, :, 4])
    guid_index = lax.axis_index("guid")
    half_width = latent.shape[2]
    own_start = guid_index * half_width
    other_start = (1 - guid_index) * half_width
    whole_velocity = jnp.einsum(
        "prd,dc->prc", final_in, full_head, preferred_element_type=jnp.float32
    )
    own_velocity = lax.dynamic_slice_in_dim(whole_velocity, own_start, half_width, 2)
    partner_part = lax.dynamic_slice_in_dim(whole_velocity, other_start, half_width, 2)
    other_velocity = partner(partner_part.astype(jnp.bfloat16), "guid", 0).astype(
        partner_part.dtype
    )
    cond_velocity = jnp.where(guid_index == 0, own_velocity, other_velocity)
    free_velocity = jnp.where(guid_index == 0, other_velocity, own_velocity)
    guided = free_velocity + guide_scale * (cond_velocity - free_velocity)
    step_value = step[0].astype(jnp.float32)
    advanced = latent + (sigma_level(step_value + 1.0) - sigma_level(step_value)) * guided
    return (advanced, guided)


def solution(mesh):
    shape = mesh.devices.shape
    cores = 2
    fine = jax.sharding.Mesh(
        mesh.devices.reshape(shape[0], shape[1] // cores, cores, shape[2]),
        ("guid", "xlo", "core", "seq"),
    )
    req = ("xlo", "core")
    every = ("guid", "xlo", "core", "seq")
    placed = (
        P("guid", req, "seq", None),
        P("guid", req, "seq", None),
        P("guid", req, None, None),
        P("guid", req, None, None),
        P(every, None),
        P(every, None),
        P(every, None),
        P(every, None),
        P("guid", req),
        P(req, "seq", "guid"),
        P(),
    )
    return jax.shard_map(
        local,
        mesh=fine,
        in_specs=placed,
        out_specs=(P(req, "seq", "guid"), P(req, "seq", "guid")),
        check_vma=False,
    )
```

```python
import jax
import jax.numpy as jnp
from jax import lax
from jax.sharding import PartitionSpec as P
from jax.experimental import pallas as pl
from jax.experimental.pallas import tpu as pltpu

HD = 64
STEPS = 28


norm_epsilon = 1e-06
flow_shift = 3.0
guide_scale = 4.5


def partner(value, axis, bit):
    mask = 2**bit
    pairs = [(source, source ^ mask) for source in range(lax.axis_size(axis))]
    return lax.ppermute(value, axis, pairs)


def modulate(values_in, shift_vec, scale_vec):
    values_in = values_in.astype(jnp.float32)
    average = jnp.mean(values_in, axis=-1, keepdims=True)
    variance = jnp.mean((values_in - average) ** 2, axis=-1, keepdims=True)
    normed = (values_in - average) * lax.rsqrt(variance + norm_epsilon)
    return (normed * (1.0 + scale_vec[..., None, :]) + shift_vec[..., None, :]).astype(jnp.bfloat16)


def sigma_level(step_value):
    remaining = 1.0 - step_value / STEPS
    return flow_shift * remaining / (1.0 + (flow_shift - 1.0) * remaining)


def attend_kernel(len_ref, q_ref, ki_ref, vi_ref, kt_ref, vt_ref, o_ref):
    length = len_ref[pl.program_id(0)]
    q = q_ref[0]
    dims = (((1,), (1,)), ((), ()))
    s_img = lax.dot_general(q, ki_ref[0], dims, preferred_element_type=jnp.float32) * 0.125
    s_txt = lax.dot_general(q, kt_ref[0], dims, preferred_element_type=jnp.float32) * 0.125
    col = lax.broadcasted_iota(jnp.int32, s_txt.shape, 1)
    s_txt = jnp.where(col < length, s_txt, -1e30)
    highest = jnp.maximum(
        jnp.max(s_img, axis=1, keepdims=True), jnp.max(s_txt, axis=1, keepdims=True)
    )
    e_img = jnp.exp(s_img - highest)
    e_txt = jnp.exp(s_txt - highest)
    totals = jnp.sum(e_img, axis=1, keepdims=True) + jnp.sum(e_txt, axis=1, keepdims=True)
    acc = jnp.dot(
        e_img.astype(jnp.bfloat16), vi_ref[0], preferred_element_type=jnp.float32
    ) + jnp.dot(e_txt.astype(jnp.bfloat16), vt_ref[0], preferred_element_type=jnp.float32)
    o_ref[0] = (acc / totals).astype(o_ref.dtype)


def attend(lengths, q, k_img, v_img, k_txt, v_txt, block=256):
    batch, rows, width = q.shape
    n_img = k_img.shape[1]
    n_txt = k_txt.shape[1]
    flops = 4 * batch * rows * (n_img + n_txt) * width
    moved = 2 * (q.size * 2 + k_img.size * 2 + k_txt.size * 2)
    return pl.pallas_call(
        attend_kernel,
        grid=(batch, rows // block),
        in_specs=[
            pl.BlockSpec(memory_space=pltpu.SMEM),
            pl.BlockSpec((1, block, width), lambda b, i: (b, i, 0)),
            pl.BlockSpec((1, n_img, width), lambda b, i: (b, 0, 0)),
            pl.BlockSpec((1, n_img, width), lambda b, i: (b, 0, 0)),
            pl.BlockSpec((1, n_txt, width), lambda b, i: (b, 0, 0)),
            pl.BlockSpec((1, n_txt, width), lambda b, i: (b, 0, 0)),
        ],
        out_specs=pl.BlockSpec((1, block, width), lambda b, i: (b, i, 0)),
        out_shape=jax.ShapeDtypeStruct(q.shape, jnp.bfloat16),
        cost_estimate=pl.CostEstimate(
            flops=flops, transcendentals=batch * rows * (n_img + n_txt), bytes_accessed=moved
        ),
    )(lengths, q, k_img, v_img, k_txt, v_txt)


def block(
    img_hidden,
    txt_hidden,
    img_mod,
    txt_mod,
    w_img_qkv,
    w_txt_qkv,
    w_out,
    w_head,
    text_lengths,
    latent,
    step,
):
    all_axes = ("guid", "xlo", "core", "seq")
    prompts = img_hidden.shape[1]
    img_rows = img_hidden.shape[2]
    txt_rows = txt_hidden.shape[2]
    model_width = img_hidden.shape[3]
    nseq = lax.axis_size("seq")

    attn_width = w_img_qkv.shape[1] // 3
    out_rows, out_cols = w_out.shape
    head_rows, head_cols = w_head.shape
    local_rows = w_img_qkv.shape[0]
    head_flat = w_head.reshape(1, head_rows * head_cols)
    head_flat = jnp.pad(head_flat, ((0, 0), (0, out_cols - head_rows * head_cols)))
    tail = jnp.concatenate([w_out, head_flat], axis=0)
    tail_width = tail.size // local_rows
    img_width = w_img_qkv.shape[1]
    txt_width = w_txt_qkv.shape[1] - attn_width
    local_all = jnp.concatenate(
        [w_img_qkv, w_txt_qkv[:, attn_width:], tail.reshape(local_rows, tail_width)], axis=1
    )
    gathered = lax.all_gather(local_all, all_axes, axis=0, tiled=False)
    full_all = gathered.reshape(-1, local_all.shape[1])
    full_img = full_all[:, :img_width]
    full_txt = full_all[:, img_width : img_width + txt_width]
    packed = full_all[:, img_width + txt_width :].reshape(-1, out_rows + 1, out_cols)
    full_out = packed[:, :out_rows].reshape(-1, out_cols)
    full_head = packed[:, out_rows, : head_rows * head_cols].reshape(-1, head_cols)

    image_in = modulate(img_hidden[0], img_mod[0, :, 0], img_mod[0, :, 1])
    text_in = modulate(txt_hidden[0], txt_mod[0, :, 0], txt_mod[0, :, 1])
    head_count = attn_width // HD
    per_dev = head_count // nseq
    qkv_image = jnp.einsum(
        "prd,de->pre", image_in, full_img, preferred_element_type=jnp.float32
    ).astype(jnp.bfloat16)
    qkv_text = jnp.einsum(
        "prd,de->pre", text_in, full_txt, preferred_element_type=jnp.float32
    ).astype(jnp.bfloat16)

    img_split = qkv_image.reshape(prompts, img_rows, 3, nseq, per_dev * HD)
    img_heads = lax.all_to_all(img_split, "seq", 3, 1, tiled=True)
    txt_split = qkv_text.reshape(prompts, txt_rows, 2, nseq, per_dev * HD)
    txt_heads = lax.all_to_all(txt_split, "seq", 3, 1, tiled=True)
    all_img = img_heads.shape[1]

    assert per_dev == 1
    lengths = text_lengths[0]
    mixture = attend(
        lengths,
        img_heads[:, :, 0, 0],
        img_heads[:, :, 1, 0],
        img_heads[:, :, 2, 0],
        txt_heads[:, :, 0, 0],
        txt_heads[:, :, 1, 0],
    )
    head_out = mixture.reshape(prompts, all_img, 1, per_dev * HD)
    token_out = lax.all_to_all(head_out, "seq", 1, 2, tiled=True)
    attended = token_out.reshape(prompts * img_rows, attn_width)

    projected = jnp.dot(attended, full_out, preferred_element_type=jnp.float32)
    residual = img_hidden[0].astype(jnp.float32) + img_mod[0, :, 2][:, None, :] * projected.reshape(
        prompts, img_rows, model_width
    )
    final_in = modulate(residual, img_mod[0, :, 3], img_mod[0, :, 4])
    guid_index = lax.axis_index("guid")
    half_width = latent.shape[2]
    own_start = guid_index * half_width
    other_start = (1 - guid_index) * half_width
    whole_velocity = jnp.einsum(
        "prd,dc->prc", final_in, full_head, preferred_element_type=jnp.float32
    )
    own_velocity = lax.dynamic_slice_in_dim(whole_velocity, own_start, half_width, 2)
    partner_part = lax.dynamic_slice_in_dim(whole_velocity, other_start, half_width, 2)
    other_velocity = partner(partner_part.astype(jnp.bfloat16), "guid", 0).astype(
        partner_part.dtype
    )
    cond_velocity = jnp.where(guid_index == 0, own_velocity, other_velocity)
    free_velocity = jnp.where(guid_index == 0, other_velocity, own_velocity)
    guided = free_velocity + guide_scale * (cond_velocity - free_velocity)
    step_value = step[0].astype(jnp.float32)
    advanced = latent + (sigma_level(step_value + 1.0) - sigma_level(step_value)) * guided
    return (advanced, guided)


def solution(mesh):
    shape = mesh.devices.shape
    cores = 2
    fine = jax.sharding.Mesh(
        mesh.devices.reshape(shape[0], shape[1] // cores, cores, shape[2]),
        ("guid", "xlo", "core", "seq"),
    )
    req = ("xlo", "core")
    every = ("guid", "xlo", "core", "seq")
    placed = (
        P("guid", req, "seq", None),
        P("guid", req, "seq", None),
        P("guid", req, None, None),
        P("guid", req, None, None),
        P(every, None),
        P(every, None),
        P(every, None),
        P(every, None),
        P("guid", req),
        P(req, "seq", "guid"),
        P(),
    )
    return jax.shard_map(
        block,
        mesh=fine,
        in_specs=placed,
        out_specs=(P(req, "seq", "guid"), P(req, "seq", "guid")),
        check_vma=False,
    )
```

```python
import jax
import jax.numpy as jnp
from jax import lax
from jax.sharding import PartitionSpec as P
from jax.experimental import pallas as pl
from jax.experimental.pallas import tpu as pltpu

HD = 64
STEPS = 28


norm_epsilon = 1e-06
flow_shift = 3.0
guide_scale = 4.5


def partner(value, axis, bit):
    mask = 2**bit
    pairs = [(source, source ^ mask) for source in range(lax.axis_size(axis))]
    return lax.ppermute(value, axis, pairs)


def modulate(values_in, shift_vec, scale_vec):
    values_in = values_in.astype(jnp.float32)
    average = jnp.mean(values_in, axis=-1, keepdims=True)
    variance = jnp.mean((values_in - average) ** 2, axis=-1, keepdims=True)
    normed = (values_in - average) * lax.rsqrt(variance + norm_epsilon)
    return (normed * (1.0 + scale_vec[..., None, :]) + shift_vec[..., None, :]).astype(jnp.bfloat16)


def sigma_level(step_value):
    remaining = 1.0 - step_value / STEPS
    return flow_shift * remaining / (1.0 + (flow_shift - 1.0) * remaining)


def attend_kernel(len_ref, q_ref, ki_ref, vi_ref, kt_ref, vt_ref, o_ref):
    length = len_ref[pl.program_id(0)]
    width = q_ref.shape[-1]
    q = q_ref[...].reshape(-1, width)
    k_img = ki_ref[...].reshape(-1, width)
    v_img = vi_ref[...].reshape(-1, width)
    dims = (((1,), (1,)), ((), ()))
    s_img = lax.dot_general(q, k_img, dims, preferred_element_type=jnp.float32) * 0.125
    s_txt = lax.dot_general(q, kt_ref[0], dims, preferred_element_type=jnp.float32) * 0.125
    col = lax.broadcasted_iota(jnp.int32, s_txt.shape, 1)
    s_txt = jnp.where(col < length, s_txt, -1e30)
    highest = jnp.maximum(
        jnp.max(s_img, axis=1, keepdims=True), jnp.max(s_txt, axis=1, keepdims=True)
    )
    e_img = jnp.exp(s_img - highest)
    e_txt = jnp.exp(s_txt - highest)
    totals = jnp.sum(e_img, axis=1, keepdims=True) + jnp.sum(e_txt, axis=1, keepdims=True)
    acc = jnp.dot(
        e_img.astype(jnp.bfloat16), v_img, preferred_element_type=jnp.float32
    ) + jnp.dot(e_txt.astype(jnp.bfloat16), vt_ref[0], preferred_element_type=jnp.float32)
    o_ref[0] = (acc / totals).astype(o_ref.dtype)


def attend(lengths, img_parts, k_txt, v_txt, block=256):
    sources, batch, _, src_rows, width = img_parts.shape
    rows = sources * src_rows
    n_txt = k_txt.shape[1]
    per_block = block // src_rows
    flops = 4 * batch * rows * (rows + n_txt) * width
    moved = 2 * (img_parts.size + k_txt.size * 2 + batch * rows * width)
    whole = (sources, 1, 1, src_rows, width)
    return pl.pallas_call(
        attend_kernel,
        grid=(batch, rows // block),
        in_specs=[
            pl.BlockSpec(memory_space=pltpu.SMEM),
            pl.BlockSpec((per_block, 1, 1, src_rows, width), lambda b, i: (i, b, 0, 0, 0)),
            pl.BlockSpec(whole, lambda b, i: (0, b, 1, 0, 0)),
            pl.BlockSpec(whole, lambda b, i: (0, b, 2, 0, 0)),
            pl.BlockSpec((1, n_txt, width), lambda b, i: (b, 0, 0)),
            pl.BlockSpec((1, n_txt, width), lambda b, i: (b, 0, 0)),
        ],
        out_specs=pl.BlockSpec((1, block, width), lambda b, i: (b, i, 0)),
        out_shape=jax.ShapeDtypeStruct((batch, rows, width), jnp.bfloat16),
        cost_estimate=pl.CostEstimate(
            flops=flops, transcendentals=batch * rows * (rows + n_txt), bytes_accessed=moved
        ),
    )(lengths, img_parts, img_parts, img_parts, k_txt, v_txt)


def block(
    img_hidden,
    txt_hidden,
    img_mod,
    txt_mod,
    w_img_qkv,
    w_txt_qkv,
    w_out,
    w_head,
    text_lengths,
    latent,
    step,
):
    all_axes = ("guid", "xlo", "core", "seq")
    prompts = img_hidden.shape[1]
    img_rows = img_hidden.shape[2]
    txt_rows = txt_hidden.shape[2]
    model_width = img_hidden.shape[3]
    nseq = lax.axis_size("seq")

    attn_width = w_img_qkv.shape[1] // 3
    out_rows, out_cols = w_out.shape
    head_rows, head_cols = w_head.shape
    local_rows = w_img_qkv.shape[0]
    head_flat = w_head.reshape(1, head_rows * head_cols)
    head_flat = jnp.pad(head_flat, ((0, 0), (0, out_cols - head_rows * head_cols)))
    tail = jnp.concatenate([w_out, head_flat], axis=0)
    tail_width = tail.size // local_rows
    img_width = w_img_qkv.shape[1]
    txt_width = w_txt_qkv.shape[1] - attn_width
    local_all = jnp.concatenate(
        [w_img_qkv, w_txt_qkv[:, attn_width:], tail.reshape(local_rows, tail_width)], axis=1
    )
    gathered = lax.all_gather(local_all, all_axes, axis=0, tiled=False)
    full_all = gathered.reshape(-1, local_all.shape[1])
    full_img = full_all[:, :img_width]
    full_txt = full_all[:, img_width : img_width + txt_width]
    packed = full_all[:, img_width + txt_width :].reshape(-1, out_rows + 1, out_cols)
    full_out = packed[:, :out_rows].reshape(-1, out_cols)
    full_head = packed[:, out_rows, : head_rows * head_cols].reshape(-1, head_cols)

    image_in = modulate(img_hidden[0], img_mod[0, :, 0], img_mod[0, :, 1])
    text_in = modulate(txt_hidden[0], txt_mod[0, :, 0], txt_mod[0, :, 1])
    head_count = attn_width // HD
    per_dev = head_count // nseq
    qkv_image = jnp.einsum(
        "prd,de->pre", image_in, full_img, preferred_element_type=jnp.float32
    ).astype(jnp.bfloat16)
    qkv_text = jnp.einsum(
        "prd,de->pre", text_in, full_txt, preferred_element_type=jnp.float32
    ).astype(jnp.bfloat16)

    img_split = qkv_image.reshape(prompts, img_rows, 3, nseq, per_dev * HD)
    img_heads = lax.all_to_all(img_split, "seq", 3, 1, tiled=True)
    txt_split = qkv_text.reshape(prompts, txt_rows, 2, nseq, per_dev * HD)
    txt_heads = lax.all_to_all(txt_split, "seq", 3, 1, tiled=True)
    all_img = img_heads.shape[1]

    assert per_dev == 1
    lengths = text_lengths[0]
    img_parts = jnp.transpose(
        img_heads.reshape(prompts, nseq, img_rows, 3, HD), (1, 0, 3, 2, 4)
    )
    mixture = attend(lengths, img_parts, txt_heads[:, :, 0, 0], txt_heads[:, :, 1, 0])
    head_out = mixture.reshape(prompts, all_img, 1, per_dev * HD)
    token_out = lax.all_to_all(head_out, "seq", 1, 2, tiled=True)
    attended = token_out.reshape(prompts * img_rows, attn_width)

    projected = jnp.dot(attended, full_out, preferred_element_type=jnp.float32)
    residual = img_hidden[0].astype(jnp.float32) + img_mod[0, :, 2][:, None, :] * projected.reshape(
        prompts, img_rows, model_width
    )
    final_in = modulate(residual, img_mod[0, :, 3], img_mod[0, :, 4])
    guid_index = lax.axis_index("guid")
    half_width = latent.shape[2]
    own_start = guid_index * half_width
    other_start = (1 - guid_index) * half_width
    whole_velocity = jnp.einsum(
        "prd,dc->prc", final_in, full_head, preferred_element_type=jnp.float32
    )
    own_velocity = lax.dynamic_slice_in_dim(whole_velocity, own_start, half_width, 2)
    partner_part = lax.dynamic_slice_in_dim(whole_velocity, other_start, half_width, 2)
    other_velocity = partner(partner_part.astype(jnp.bfloat16), "guid", 0).astype(
        partner_part.dtype
    )
    cond_velocity = jnp.where(guid_index == 0, own_velocity, other_velocity)
    free_velocity = jnp.where(guid_index == 0, other_velocity, own_velocity)
    guided = free_velocity + guide_scale * (cond_velocity - free_velocity)
    step_value = step[0].astype(jnp.float32)
    advanced = latent + (sigma_level(step_value + 1.0) - sigma_level(step_value)) * guided
    return (advanced, guided)


def solution(mesh):
    shape = mesh.devices.shape
    cores = 2
    fine = jax.sharding.Mesh(
        mesh.devices.reshape(shape[0], shape[1] // cores, cores, shape[2]),
        ("guid", "xlo", "core", "seq"),
    )
    req = ("xlo", "core")
    every = ("guid", "xlo", "core", "seq")
    placed = (
        P("guid", req, "seq", None),
        P("guid", req, "seq", None),
        P("guid", req, None, None),
        P("guid", req, None, None),
        P(every, None),
        P(every, None),
        P(every, None),
        P(every, None),
        P("guid", req),
        P(req, "seq", "guid"),
        P(),
    )
    return jax.shard_map(
        block,
        mesh=fine,
        in_specs=placed,
        out_specs=(P(req, "seq", "guid"), P(req, "seq", "guid")),
        check_vma=False,
    )
```

```python
import jax
import jax.numpy as jnp
from jax import lax
from jax.sharding import PartitionSpec as P
from jax.experimental import pallas as pl
from jax.experimental.pallas import tpu as pltpu

HD = 64
STEPS = 28


norm_epsilon = 1e-06
flow_shift = 3.0
guide_scale = 4.5


def partner(value, axis, bit):
    mask = 2**bit
    pairs = [(source, source ^ mask) for source in range(lax.axis_size(axis))]
    return lax.ppermute(value, axis, pairs)


def modulate(values_in, shift_vec, scale_vec):
    values_in = values_in.astype(jnp.float32)
    average = jnp.mean(values_in, axis=-1, keepdims=True)
    variance = jnp.mean((values_in - average) ** 2, axis=-1, keepdims=True)
    normed = (values_in - average) * lax.rsqrt(variance + norm_epsilon)
    return (normed * (1.0 + scale_vec[..., None, :]) + shift_vec[..., None, :]).astype(jnp.bfloat16)


def sigma_level(step_value):
    remaining = 1.0 - step_value / STEPS
    return flow_shift * remaining / (1.0 + (flow_shift - 1.0) * remaining)


def attend_kernel(len_ref, q_ref, ki_ref, vi_ref, kt_ref, vt_ref, o_ref):
    length = len_ref[pl.program_id(0)]
    width = q_ref.shape[-1]
    q = q_ref[...].reshape(-1, width)
    k_img = ki_ref[...].reshape(-1, width)
    v_img = vi_ref[...].reshape(-1, width)
    dims = (((1,), (1,)), ((), ()))
    s_img = lax.dot_general(q, k_img, dims, preferred_element_type=jnp.float32) * 0.125
    s_txt = lax.dot_general(q, kt_ref[0], dims, preferred_element_type=jnp.float32) * 0.125
    col = lax.broadcasted_iota(jnp.int32, s_txt.shape, 1)
    s_txt = jnp.where(col < length, s_txt, -1e30)
    highest = jnp.maximum(
        jnp.max(s_img, axis=1, keepdims=True), jnp.max(s_txt, axis=1, keepdims=True)
    )
    e_img = jnp.exp(s_img - highest)
    e_txt = jnp.exp(s_txt - highest)
    totals = jnp.sum(e_img, axis=1, keepdims=True) + jnp.sum(e_txt, axis=1, keepdims=True)
    acc = jnp.dot(
        e_img.astype(jnp.bfloat16), v_img, preferred_element_type=jnp.float32
    ) + jnp.dot(e_txt.astype(jnp.bfloat16), vt_ref[0], preferred_element_type=jnp.float32)
    o_ref[0] = (acc / totals).astype(o_ref.dtype)


def attend(lengths, img_parts, k_txt, v_txt, block=256):
    sources, batch, _, src_rows, width = img_parts.shape
    rows = sources * src_rows
    n_txt = k_txt.shape[1]
    per_block = block // src_rows
    flops = 4 * batch * rows * (rows + n_txt) * width
    moved = 2 * (img_parts.size + k_txt.size * 2 + batch * rows * width)
    whole = (sources, 1, 1, src_rows, width)
    return pl.pallas_call(
        attend_kernel,
        grid=(batch, rows // block),
        in_specs=[
            pl.BlockSpec(memory_space=pltpu.SMEM),
            pl.BlockSpec((per_block, 1, 1, src_rows, width), lambda b, i: (i, b, 0, 0, 0)),
            pl.BlockSpec(whole, lambda b, i: (0, b, 1, 0, 0)),
            pl.BlockSpec(whole, lambda b, i: (0, b, 2, 0, 0)),
            pl.BlockSpec((1, n_txt, width), lambda b, i: (b, 0, 0)),
            pl.BlockSpec((1, n_txt, width), lambda b, i: (b, 0, 0)),
        ],
        out_specs=pl.BlockSpec((1, block, width), lambda b, i: (b, i, 0)),
        out_shape=jax.ShapeDtypeStruct((batch, rows, width), jnp.bfloat16),
        cost_estimate=pl.CostEstimate(
            flops=flops, transcendentals=batch * rows * (rows + n_txt), bytes_accessed=moved
        ),
    )(lengths, img_parts, img_parts, img_parts, k_txt, v_txt)


def block(
    img_hidden,
    txt_hidden,
    img_mod,
    txt_mod,
    w_img_qkv,
    w_txt_qkv,
    w_out,
    w_head,
    text_lengths,
    latent,
    step,
):
    all_axes = ("guid", "xlo", "core", "seq")
    prompts = img_hidden.shape[1]
    img_rows = img_hidden.shape[2]
    txt_rows = txt_hidden.shape[2]
    model_width = img_hidden.shape[3]
    nseq = lax.axis_size("seq")

    attn_width = w_img_qkv.shape[1] // 3
    out_rows, out_cols = w_out.shape
    head_rows, head_cols = w_head.shape
    local_rows = w_img_qkv.shape[0]
    head_flat = w_head.reshape(1, head_rows * head_cols)
    head_flat = jnp.pad(head_flat, ((0, 0), (0, out_cols - head_rows * head_cols)))
    tail = jnp.concatenate([w_out, head_flat], axis=0)
    tail_width = tail.size // local_rows
    img_width = w_img_qkv.shape[1]
    txt_width = w_txt_qkv.shape[1] - attn_width
    local_all = jnp.concatenate(
        [w_img_qkv, w_txt_qkv[:, attn_width:], tail.reshape(local_rows, tail_width)], axis=1
    )
    gathered = lax.all_gather(local_all, all_axes, axis=0, tiled=False)
    full_all = gathered.reshape(-1, local_all.shape[1])
    full_img = full_all[:, :img_width]
    full_txt = full_all[:, img_width : img_width + txt_width]
    packed = full_all[:, img_width + txt_width :].reshape(-1, out_rows + 1, out_cols)
    full_out = packed[:, :out_rows].reshape(-1, out_cols)
    full_head = packed[:, out_rows, : head_rows * head_cols].reshape(-1, head_cols)

    image_in = modulate(img_hidden[0], img_mod[0, :, 0], img_mod[0, :, 1])
    text_in = modulate(txt_hidden[0], txt_mod[0, :, 0], txt_mod[0, :, 1])
    head_count = attn_width // HD
    per_dev = head_count // nseq
    qkv_image = jnp.einsum(
        "prd,de->pre", image_in, full_img, preferred_element_type=jnp.float32
    ).astype(jnp.bfloat16)
    qkv_text = jnp.einsum(
        "prd,de->pre", text_in, full_txt, preferred_element_type=jnp.float32
    ).astype(jnp.bfloat16)

    img_split = jnp.transpose(
        qkv_image.reshape(prompts, img_rows, 3, nseq, per_dev * HD), (3, 0, 2, 1, 4)
    )
    img_parts = lax.all_to_all(img_split, "seq", 0, 0, tiled=True)
    txt_split = qkv_text.reshape(prompts, txt_rows, 2, nseq, per_dev * HD)
    txt_heads = lax.all_to_all(txt_split, "seq", 3, 1, tiled=True)
    all_img = nseq * img_rows

    assert per_dev == 1
    lengths = text_lengths[0]
    mixture = attend(lengths, img_parts, txt_heads[:, :, 0, 0], txt_heads[:, :, 1, 0])
    head_out = mixture.reshape(prompts, all_img, 1, per_dev * HD)
    token_out = lax.all_to_all(head_out, "seq", 1, 2, tiled=True)
    attended = token_out.reshape(prompts * img_rows, attn_width)

    projected = jnp.dot(attended, full_out, preferred_element_type=jnp.float32)
    residual = img_hidden[0].astype(jnp.float32) + img_mod[0, :, 2][:, None, :] * projected.reshape(
        prompts, img_rows, model_width
    )
    final_in = modulate(residual, img_mod[0, :, 3], img_mod[0, :, 4])
    guid_index = lax.axis_index("guid")
    half_width = latent.shape[2]
    own_start = guid_index * half_width
    other_start = (1 - guid_index) * half_width
    whole_velocity = jnp.einsum(
        "prd,dc->prc", final_in, full_head, preferred_element_type=jnp.float32
    )
    own_velocity = lax.dynamic_slice_in_dim(whole_velocity, own_start, half_width, 2)
    partner_part = lax.dynamic_slice_in_dim(whole_velocity, other_start, half_width, 2)
    other_velocity = partner(partner_part.astype(jnp.bfloat16), "guid", 0).astype(
        partner_part.dtype
    )
    cond_velocity = jnp.where(guid_index == 0, own_velocity, other_velocity)
    free_velocity = jnp.where(guid_index == 0, other_velocity, own_velocity)
    guided = free_velocity + guide_scale * (cond_velocity - free_velocity)
    step_value = step[0].astype(jnp.float32)
    advanced = latent + (sigma_level(step_value + 1.0) - sigma_level(step_value)) * guided
    return (advanced, guided)


def solution(mesh):
    shape = mesh.devices.shape
    cores = 2
    fine = jax.sharding.Mesh(
        mesh.devices.reshape(shape[0], shape[1] // cores, cores, shape[2]),
        ("guid", "xlo", "core", "seq"),
    )
    req = ("xlo", "core")
    every = ("guid", "xlo", "core", "seq")
    placed = (
        P("guid", req, "seq", None),
        P("guid", req, "seq", None),
        P("guid", req, None, None),
        P("guid", req, None, None),
        P(every, None),
        P(every, None),
        P(every, None),
        P(every, None),
        P("guid", req),
        P(req, "seq", "guid"),
        P(),
    )
    return jax.shard_map(
        block,
        mesh=fine,
        in_specs=placed,
        out_specs=(P(req, "seq", "guid"), P(req, "seq", "guid")),
        check_vma=False,
    )
```

```python
import jax
import jax.numpy as jnp
from jax import lax
from jax.sharding import PartitionSpec as P
from jax.experimental import pallas as pl
from jax.experimental.pallas import tpu as pltpu

HD = 64
STEPS = 28


norm_epsilon = 1e-06
flow_shift = 3.0
guide_scale = 4.5


def partner(value, axis, bit):
    mask = 2**bit
    pairs = [(source, source ^ mask) for source in range(lax.axis_size(axis))]
    return lax.ppermute(value, axis, pairs)


def modulate(values_in, shift_vec, scale_vec):
    values_in = values_in.astype(jnp.float32)
    average = jnp.mean(values_in, axis=-1, keepdims=True)
    variance = jnp.mean((values_in - average) ** 2, axis=-1, keepdims=True)
    normed = (values_in - average) * lax.rsqrt(variance + norm_epsilon)
    return (normed * (1.0 + scale_vec[..., None, :]) + shift_vec[..., None, :]).astype(jnp.bfloat16)


def sigma_level(step_value):
    remaining = 1.0 - step_value / STEPS
    return flow_shift * remaining / (1.0 + (flow_shift - 1.0) * remaining)


def attend_kernel(len_ref, q_ref, ki_ref, vi_ref, kt_ref, vt_ref, o_ref):
    length = len_ref[pl.program_id(0)]
    width = q_ref.shape[-1]
    q = q_ref[...].reshape(-1, width)
    k_img = ki_ref[...].reshape(-1, width)
    v_img = vi_ref[...].reshape(-1, width)
    dims = (((1,), (1,)), ((), ()))
    s_img = lax.dot_general(q, k_img, dims, preferred_element_type=jnp.float32) * 0.125
    s_txt = lax.dot_general(q, kt_ref[0], dims, preferred_element_type=jnp.float32) * 0.125
    col = lax.broadcasted_iota(jnp.int32, s_txt.shape, 1)
    s_txt = jnp.where(col < length, s_txt, -1e30)
    highest = jnp.maximum(
        jnp.max(s_img, axis=1, keepdims=True), jnp.max(s_txt, axis=1, keepdims=True)
    )
    e_img = jnp.exp(s_img - highest)
    e_txt = jnp.exp(s_txt - highest)
    totals = jnp.sum(e_img, axis=1, keepdims=True) + jnp.sum(e_txt, axis=1, keepdims=True)
    acc = jnp.dot(
        e_img.astype(jnp.bfloat16), v_img, preferred_element_type=jnp.float32
    ) + jnp.dot(e_txt.astype(jnp.bfloat16), vt_ref[0], preferred_element_type=jnp.float32)
    o_ref[:, 0] = (acc / totals).astype(o_ref.dtype).reshape(o_ref.shape[0], -1, width)


def attend(lengths, img_parts, k_txt, v_txt, block=256):
    sources, batch, _, src_rows, width = img_parts.shape
    rows = sources * src_rows
    n_txt = k_txt.shape[1]
    per_block = block // src_rows
    flops = 4 * batch * rows * (rows + n_txt) * width
    moved = 2 * (img_parts.size + k_txt.size * 2 + batch * rows * width)
    whole = (sources, 1, 1, src_rows, width)
    return pl.pallas_call(
        attend_kernel,
        grid=(batch, rows // block),
        in_specs=[
            pl.BlockSpec(memory_space=pltpu.SMEM),
            pl.BlockSpec((per_block, 1, 1, src_rows, width), lambda b, i: (i, b, 0, 0, 0)),
            pl.BlockSpec(whole, lambda b, i: (0, b, 1, 0, 0)),
            pl.BlockSpec(whole, lambda b, i: (0, b, 2, 0, 0)),
            pl.BlockSpec((1, n_txt, width), lambda b, i: (b, 0, 0)),
            pl.BlockSpec((1, n_txt, width), lambda b, i: (b, 0, 0)),
        ],
        out_specs=pl.BlockSpec((per_block, 1, src_rows, width), lambda b, i: (i, b, 0, 0)),
        out_shape=jax.ShapeDtypeStruct((sources, batch, src_rows, width), jnp.bfloat16),
        cost_estimate=pl.CostEstimate(
            flops=flops, transcendentals=batch * rows * (rows + n_txt), bytes_accessed=moved
        ),
    )(lengths, img_parts, img_parts, img_parts, k_txt, v_txt)


def block(
    img_hidden,
    txt_hidden,
    img_mod,
    txt_mod,
    w_img_qkv,
    w_txt_qkv,
    w_out,
    w_head,
    text_lengths,
    latent,
    step,
):
    all_axes = ("guid", "xlo", "core", "seq")
    prompts = img_hidden.shape[1]
    txt_rows = txt_hidden.shape[2]
    model_width = img_hidden.shape[3]
    nseq = lax.axis_size("seq")

    attn_width = w_img_qkv.shape[1] // 3
    out_rows, out_cols = w_out.shape
    head_rows, head_cols = w_head.shape
    local_rows = w_img_qkv.shape[0]
    head_flat = w_head.reshape(1, head_rows * head_cols)
    head_flat = jnp.pad(head_flat, ((0, 0), (0, out_cols - head_rows * head_cols)))
    tail = jnp.concatenate([w_out, head_flat], axis=0)
    tail_width = tail.size // local_rows
    img_width = w_img_qkv.shape[1]
    txt_width = w_txt_qkv.shape[1] - attn_width
    local_all = jnp.concatenate(
        [w_img_qkv, w_txt_qkv[:, attn_width:], tail.reshape(local_rows, tail_width)], axis=1
    )
    gathered = lax.all_gather(local_all, all_axes, axis=0, tiled=False)
    full_all = gathered.reshape(-1, local_all.shape[1])
    full_img = full_all[:, :img_width]
    full_txt = full_all[:, img_width : img_width + txt_width]
    packed = full_all[:, img_width + txt_width :].reshape(-1, out_rows + 1, out_cols)
    full_out = packed[:, :out_rows].reshape(-1, out_cols)
    full_head = packed[:, out_rows, : head_rows * head_cols].reshape(-1, head_cols)

    image_in = modulate(img_hidden[0], img_mod[0, :, 0], img_mod[0, :, 1])
    text_in = modulate(txt_hidden[0], txt_mod[0, :, 0], txt_mod[0, :, 1])
    head_count = attn_width // HD
    per_dev = head_count // nseq
    img_split = jnp.einsum(
        "prd,dthe->hptre",
        image_in,
        full_img.reshape(-1, 3, nseq, per_dev * HD),
        preferred_element_type=jnp.float32,
    ).astype(jnp.bfloat16)
    qkv_text = jnp.einsum(
        "prd,de->pre", text_in, full_txt, preferred_element_type=jnp.float32
    ).astype(jnp.bfloat16)

    img_parts = lax.all_to_all(img_split, "seq", 0, 0, tiled=True)
    txt_split = qkv_text.reshape(prompts, txt_rows, 2, nseq, per_dev * HD)
    txt_heads = lax.all_to_all(txt_split, "seq", 3, 1, tiled=True)

    assert per_dev == 1
    lengths = text_lengths[0]
    mixture = attend(lengths, img_parts, txt_heads[:, :, 0, 0], txt_heads[:, :, 1, 0])
    head_parts = lax.all_to_all(mixture, "seq", 0, 0, tiled=True)
    projected = jnp.einsum(
        "hprd,hdc->prc",
        head_parts,
        full_out.reshape(nseq, per_dev * HD, model_width),
        preferred_element_type=jnp.float32,
    )
    residual = img_hidden[0].astype(jnp.float32) + img_mod[0, :, 2][:, None, :] * projected
    final_in = modulate(residual, img_mod[0, :, 3], img_mod[0, :, 4])
    guid_index = lax.axis_index("guid")
    half_width = latent.shape[2]
    own_start = guid_index * half_width
    other_start = (1 - guid_index) * half_width
    whole_velocity = jnp.einsum(
        "prd,dc->prc", final_in, full_head, preferred_element_type=jnp.float32
    )
    own_velocity = lax.dynamic_slice_in_dim(whole_velocity, own_start, half_width, 2)
    partner_part = lax.dynamic_slice_in_dim(whole_velocity, other_start, half_width, 2)
    other_velocity = partner(partner_part.astype(jnp.bfloat16), "guid", 0).astype(
        partner_part.dtype
    )
    cond_velocity = jnp.where(guid_index == 0, own_velocity, other_velocity)
    free_velocity = jnp.where(guid_index == 0, other_velocity, own_velocity)
    guided = free_velocity + guide_scale * (cond_velocity - free_velocity)
    step_value = step[0].astype(jnp.float32)
    advanced = latent + (sigma_level(step_value + 1.0) - sigma_level(step_value)) * guided
    return (advanced, guided)


def solution(mesh):
    shape = mesh.devices.shape
    cores = 2
    fine = jax.sharding.Mesh(
        mesh.devices.reshape(shape[0], shape[1] // cores, cores, shape[2]),
        ("guid", "xlo", "core", "seq"),
    )
    req = ("xlo", "core")
    every = ("guid", "xlo", "core", "seq")
    placed = (
        P("guid", req, "seq", None),
        P("guid", req, "seq", None),
        P("guid", req, None, None),
        P("guid", req, None, None),
        P(every, None),
        P(every, None),
        P(every, None),
        P(every, None),
        P("guid", req),
        P(req, "seq", "guid"),
        P(),
    )
    return jax.shard_map(
        block,
        mesh=fine,
        in_specs=placed,
        out_specs=(P(req, "seq", "guid"), P(req, "seq", "guid")),
        check_vma=False,
    )
```

```python
import jax
import jax.numpy as jnp
from jax import lax
from jax.sharding import PartitionSpec as P
from jax.experimental import pallas as pl
from jax.experimental.pallas import tpu as pltpu

HD = 64
STEPS = 28


norm_epsilon = 1e-06
flow_shift = 3.0
guide_scale = 4.5


def partner(value, axis, bit):
    mask = 2**bit
    pairs = [(source, source ^ mask) for source in range(lax.axis_size(axis))]
    return lax.ppermute(value, axis, pairs)


def modulate(values_in, shift_vec, scale_vec):
    values_in = values_in.astype(jnp.float32)
    average = jnp.mean(values_in, axis=-1, keepdims=True)
    variance = jnp.mean((values_in - average) ** 2, axis=-1, keepdims=True)
    normed = (values_in - average) * lax.rsqrt(variance + norm_epsilon)
    return (normed * (1.0 + scale_vec[..., None, :]) + shift_vec[..., None, :]).astype(jnp.bfloat16)


def sigma_level(step_value):
    remaining = 1.0 - step_value / STEPS
    return flow_shift * remaining / (1.0 + (flow_shift - 1.0) * remaining)


def attend_kernel(len_ref, q_ref, ki_ref, vi_ref, kt_ref, vt_ref, o_ref):
    length = len_ref[pl.program_id(0)]
    width = q_ref.shape[-1]
    q = q_ref[...].reshape(-1, width)
    k_img = ki_ref[...].reshape(-1, width)
    v_img = vi_ref[...].reshape(-1, width)
    dims = (((1,), (1,)), ((), ()))
    s_img = lax.dot_general(q, k_img, dims, preferred_element_type=jnp.float32) * 0.125
    s_txt = lax.dot_general(q, kt_ref[0], dims, preferred_element_type=jnp.float32) * 0.125
    col = lax.broadcasted_iota(jnp.int32, s_txt.shape, 1)
    s_txt = jnp.where(col < length, s_txt, -1e30)
    highest = jnp.maximum(
        jnp.max(s_img, axis=1, keepdims=True), jnp.max(s_txt, axis=1, keepdims=True)
    )
    e_img = jnp.exp(s_img - highest)
    e_txt = jnp.exp(s_txt - highest)
    totals = jnp.sum(e_img, axis=1, keepdims=True) + jnp.sum(e_txt, axis=1, keepdims=True)
    acc = jnp.dot(
        e_img.astype(jnp.bfloat16), v_img, preferred_element_type=jnp.float32
    ) + jnp.dot(e_txt.astype(jnp.bfloat16), vt_ref[0], preferred_element_type=jnp.float32)
    o_ref[:, 0] = (acc / totals).astype(o_ref.dtype).reshape(o_ref.shape[0], -1, width)


def attend(lengths, img_parts, k_txt, v_txt, block=1024):
    sources, batch, _, src_rows, width = img_parts.shape
    rows = sources * src_rows
    n_txt = k_txt.shape[1]
    per_block = block // src_rows
    flops = 4 * batch * rows * (rows + n_txt) * width
    moved = 2 * (img_parts.size + k_txt.size * 2 + batch * rows * width)
    whole = (sources, 1, 1, src_rows, width)
    return pl.pallas_call(
        attend_kernel,
        grid=(batch, rows // block),
        in_specs=[
            pl.BlockSpec(memory_space=pltpu.SMEM),
            pl.BlockSpec((per_block, 1, 1, src_rows, width), lambda b, i: (i, b, 0, 0, 0)),
            pl.BlockSpec(whole, lambda b, i: (0, b, 1, 0, 0)),
            pl.BlockSpec(whole, lambda b, i: (0, b, 2, 0, 0)),
            pl.BlockSpec((1, n_txt, width), lambda b, i: (b, 0, 0)),
            pl.BlockSpec((1, n_txt, width), lambda b, i: (b, 0, 0)),
        ],
        out_specs=pl.BlockSpec((per_block, 1, src_rows, width), lambda b, i: (i, b, 0, 0)),
        out_shape=jax.ShapeDtypeStruct((sources, batch, src_rows, width), jnp.bfloat16),
        cost_estimate=pl.CostEstimate(
            flops=flops, transcendentals=batch * rows * (rows + n_txt), bytes_accessed=moved
        ),
    )(lengths, img_parts, img_parts, img_parts, k_txt, v_txt)


def block(
    img_hidden,
    txt_hidden,
    img_mod,
    txt_mod,
    w_img_qkv,
    w_txt_qkv,
    w_out,
    w_head,
    text_lengths,
    latent,
    step,
):
    all_axes = ("guid", "xlo", "core", "seq")
    prompts = img_hidden.shape[1]
    img_rows = img_hidden.shape[2]
    txt_rows = txt_hidden.shape[2]
    model_width = img_hidden.shape[3]
    nseq = lax.axis_size("seq")

    attn_width = w_img_qkv.shape[1] // 3
    out_rows, out_cols = w_out.shape
    head_rows, head_cols = w_head.shape
    local_rows = w_img_qkv.shape[0]
    head_flat = w_head.reshape(1, head_rows * head_cols)
    head_flat = jnp.pad(head_flat, ((0, 0), (0, out_cols - head_rows * head_cols)))
    tail = jnp.concatenate([w_out, head_flat], axis=0)
    tail_width = tail.size // local_rows
    img_width = w_img_qkv.shape[1]
    txt_width = w_txt_qkv.shape[1] - attn_width
    local_all = jnp.concatenate(
        [w_img_qkv, w_txt_qkv[:, attn_width:], tail.reshape(local_rows, tail_width)], axis=1
    )
    gathered = lax.all_gather(local_all, all_axes, axis=0, tiled=False)
    full_all = gathered.reshape(-1, local_all.shape[1])
    full_img = full_all[:, :img_width]
    full_txt = full_all[:, img_width : img_width + txt_width]
    packed = full_all[:, img_width + txt_width :].reshape(-1, out_rows + 1, out_cols)
    full_out = packed[:, :out_rows].reshape(-1, out_cols)
    full_head = packed[:, out_rows, : head_rows * head_cols].reshape(-1, head_cols)

    image_in = modulate(img_hidden[0], img_mod[0, :, 0], img_mod[0, :, 1])
    text_in = modulate(txt_hidden[0], txt_mod[0, :, 0], txt_mod[0, :, 1])
    head_count = attn_width // HD
    per_dev = head_count // nseq
    qkv_image = jnp.einsum(
        "prd,de->pre", image_in, full_img, preferred_element_type=jnp.float32
    ).astype(jnp.bfloat16)
    qkv_text = jnp.einsum(
        "prd,de->pre", text_in, full_txt, preferred_element_type=jnp.float32
    ).astype(jnp.bfloat16)

    img_split = jnp.transpose(
        qkv_image.reshape(prompts, img_rows, 3, nseq, per_dev * HD), (3, 0, 2, 1, 4)
    )
    img_parts = lax.all_to_all(img_split, "seq", 0, 0, tiled=True)
    txt_split = qkv_text.reshape(prompts, txt_rows, 2, nseq, per_dev * HD)
    txt_heads = lax.all_to_all(txt_split, "seq", 3, 1, tiled=True)

    assert per_dev == 1
    lengths = text_lengths[0]
    mixture = attend(lengths, img_parts, txt_heads[:, :, 0, 0], txt_heads[:, :, 1, 0])
    head_parts = lax.all_to_all(mixture, "seq", 0, 0, tiled=True)
    projected = jnp.einsum(
        "hprd,hdc->prc",
        head_parts,
        full_out.reshape(nseq, per_dev * HD, model_width),
        preferred_element_type=jnp.float32,
    )
    residual = img_hidden[0].astype(jnp.float32) + img_mod[0, :, 2][:, None, :] * projected
    final_in = modulate(residual, img_mod[0, :, 3], img_mod[0, :, 4])
    guid_index = lax.axis_index("guid")
    half_width = latent.shape[2]
    own_start = guid_index * half_width
    other_start = (1 - guid_index) * half_width
    whole_velocity = jnp.einsum(
        "prd,dc->prc", final_in, full_head, preferred_element_type=jnp.float32
    )
    own_velocity = lax.dynamic_slice_in_dim(whole_velocity, own_start, half_width, 2)
    partner_part = lax.dynamic_slice_in_dim(whole_velocity, other_start, half_width, 2)
    other_velocity = partner(partner_part.astype(jnp.bfloat16), "guid", 0).astype(
        partner_part.dtype
    )
    cond_velocity = jnp.where(guid_index == 0, own_velocity, other_velocity)
    free_velocity = jnp.where(guid_index == 0, other_velocity, own_velocity)
    guided = free_velocity + guide_scale * (cond_velocity - free_velocity)
    step_value = step[0].astype(jnp.float32)
    advanced = latent + (sigma_level(step_value + 1.0) - sigma_level(step_value)) * guided
    return (advanced, guided)


def solution(mesh):
    shape = mesh.devices.shape
    cores = 2
    fine = jax.sharding.Mesh(
        mesh.devices.reshape(shape[0], shape[1] // cores, cores, shape[2]),
        ("guid", "xlo", "core", "seq"),
    )
    req = ("xlo", "core")
    every = ("guid", "xlo", "core", "seq")
    placed = (
        P("guid", req, "seq", None),
        P("guid", req, "seq", None),
        P("guid", req, None, None),
        P("guid", req, None, None),
        P(every, None),
        P(every, None),
        P(every, None),
        P(every, None),
        P("guid", req),
        P(req, "seq", "guid"),
        P(),
    )
    return jax.shard_map(
        block,
        mesh=fine,
        in_specs=placed,
        out_specs=(P(req, "seq", "guid"), P(req, "seq", "guid")),
        check_vma=False,
    )
```
